1024 devices in a mesh: ctx: 64 (over y, x, core), exp: 16 (over z).
Axes of the slice: x: 4, y: 8, z: 16, core: 2. Of those that a mesh axis runs over, the one named last changes fastest.
Arguments:
- queries: bfloat16 [16384, 4096], P(('ctx', 'exp')), may hold values from -1.25 to 1.25
- keys: bfloat16 [16384, 4096], P(('ctx', 'exp')), may hold values from -0.75 to 0.75
- values: bfloat16 [16384, 4096], P(('ctx', 'exp')), may hold values from -6 to 6
- out_grad: bfloat16 [16384, 4096], P(('ctx', 'exp')), may hold values from -1.5 to 1.5
- decay_rate: float32 [32], P('exp'), may hold values from 1.2207031e-06 to 0.04
- doc_lengths: int32 [8], replicated, may hold values from 1 to 8192, 16384 in all
Outputs:
- attn_out: bfloat16 [16384, 4096], P('ctx', 'exp')
- grad_queries: bfloat16 [16384, 4096], P('ctx', 'exp')
- grad_keys: bfloat16 [16384, 4096], P('ctx', 'exp')
- grad_values: bfloat16 [16384, 4096], P('ctx', 'exp')
The draws below stay inside these ranges and needn't reach their ends.
Inputs may be any that keep to these rules, and one draw needn't show every extreme that they name: `doc_lengths`: lengths of the 8 documents in order, summing to 16384; the longest is exactly 8192.
All inputs are finite; a program needn't handle non-finite values.
Results may differ from the reference program's by a relative error of at most 0.0033.
Values may be sent and summed in bfloat16 or wider, within the bound.
No kernel may reach another device: no remote copies, remote signals or barrier semaphores. Data moves between devices by JAX's collectives and lax.ppermute only.
A program may use at most 64 MiB of HBM per device.

```python
import math
import jax
import jax.numpy as jnp
import numpy as np
from jax import lax

HEADS = 32
DH = 128
GROUP = 256
DOCS = 8
SEQ = 16384


def steps_of(stream_key, shape, pieces, smallest, largest):
    factor_of = 1.0
    for axis_at, blocks in pieces:
        draws = jax.random.uniform(jax.random.fold_in(jax.random.fold_in(stream_key, 6), axis_at), (blocks,), jnp.float32, smallest / len(pieces), largest / len(pieces))
        factor_of = factor_of * jnp.repeat(jnp.exp(draws), shape[axis_at] // blocks).reshape((-1,) + (1,) * (len(shape) - 1 - axis_at))
    return factor_of


def profile(count, total, bound, slope):
    weights = [(1 << 20) // math.isqrt(rank ** slope) + 1 for rank in range(2, count + 1)]
    surplus, holding = total - bound - (count - 1), [1] * (count - 1)
    while surplus > 0:
        movable = [i for i in range(count - 1) if holding[i] < bound]
        mass, remaining = sum([weights[i] for i in movable]), surplus
        for i in movable:
            addition = min(bound - holding[i], max(1, remaining * weights[i] // mass), surplus)
            holding[i] = holding[i] + addition
            surplus = surplus - addition
    return np.array([bound] + holding)


def ragged(own_key, amount, total, most, skew):
    if amount == 2:
        one = jax.random.randint(own_key, (), max(1, total - most), min(most, total - 1) + 1)
        return jnp.stack([one, total - one])
    sizes = jnp.asarray(profile(amount, total, most, skew), jnp.int32)
    twos = (amount - 1) // 2
    source_of, taker = sizes[1:1 + 2 * twos:2], sizes[2:2 + 2 * twos:2]
    margin = jnp.minimum(source_of - 1, most - taker)
    passed = jax.random.randint(jax.random.fold_in(own_key, 1), (twos,), 0, 1 << 20) % (margin + 1)
    sizes = sizes.at[1:1 + 2 * twos:2].set(source_of - passed).at[2:2 + 2 * twos:2].set(taker + passed)
    return sizes[jax.random.permutation(jax.random.fold_in(own_key, 2), amount)]


def bell_draw(rng, extent, deviation, reach, pieces=(), kind=jnp.bfloat16):
    factor_of = steps_of(rng, extent, pieces, -0.22, 0.18) if pieces else 1.0
    result = jax.random.normal(rng, extent, jnp.float32) * deviation * factor_of
    return jnp.minimum(jnp.maximum(result, -reach), reach).astype(kind)


def setup_inputs(seed: int = 0) -> dict:
    splits = jax.random.split(jax.random.key(seed), 7)
    return {
        "queries": bell_draw(splits[0], (SEQ, HEADS * DH), (1.0 / DH ** 0.5), 1.25, ((0, 1024),)),
        "keys": bell_draw(splits[1], (SEQ, HEADS * DH), 0.05, 0.75, ((0, 1024),)),
        "values": bell_draw(splits[2], (SEQ, HEADS * DH), 1.0, 6.0, ((0, 1024),)),
        "out_grad": bell_draw(splits[3], (SEQ, HEADS * DH), 0.1, 1.5, ((0, 1024),)),
        "decay_rate": jnp.clip(jnp.exp(math.log(0.04) - 10.3972077 * jax.random.uniform(splits[4], (HEADS,), jnp.float32) ** steps_of(splits[4], (HEADS,), ((0, 16),), -0.2, 0.2)), 1.220703097715159e-06, 0.04),
        "doc_lengths": ragged(splits[5], DOCS, SEQ, SEQ // 2, 2).astype(jnp.int32),
    }


def segment_of(positions, doc_ends):
    return jnp.sum((doc_ends[None, :] <= positions[:, None]).astype(jnp.int32), axis=1)


def group_masks(group_index, doc_lengths, decays, group_len):
    doc_ends = jnp.cumsum(doc_lengths).astype(jnp.int32)
    offsets = jnp.arange(group_len, dtype=jnp.int32)
    first_row = (group_index * group_len).astype(jnp.int32)
    segment = segment_of(first_row + offsets, doc_ends)
    segment_prev = segment_of(first_row - 1 + jnp.zeros((1,), jnp.int32), doc_ends)[0]
    segment_last = segment[group_len - 1]
    enters = (segment == segment_prev).astype(jnp.float32)
    leaves = (segment == segment_last).astype(jnp.float32)
    distance = (offsets[:, None] - offsets[None, :]).astype(jnp.float32)
    allowed = (offsets[:, None] >= offsets[None, :]) & (segment[:, None] == segment[None, :])
    weights = jnp.where(allowed[None], jnp.exp(-decays[:, None, None] * jnp.maximum(distance, 0.0)[None]), 0.0)
    offsets_f = offsets.astype(jnp.float32)
    enter_w = jnp.exp(-decays[:, None] * (offsets_f + 1.0)[None]) * enters[None]
    leave_w = jnp.exp(-decays[:, None] * (group_len - 1.0 - offsets_f)[None]) * leaves[None]
    carried = jnp.exp(-decays * group_len) * (segment_last == segment_prev).astype(jnp.float32)
    return weights, enter_w, leave_w, carried


def reference(queries, keys, values, out_grad, decay_rate, doc_lengths):
    precise = lax.Precision.HIGHEST
    group_count = SEQ // GROUP
    decays = decay_rate.astype(jnp.float32)
    q_all = queries.reshape(group_count, GROUP, HEADS, DH)
    k_all = keys.reshape(group_count, GROUP, HEADS, DH)
    v_all = values.reshape(group_count, GROUP, HEADS, DH)
    g_all = out_grad.reshape(group_count, GROUP, HEADS, DH)

    def forward_step(state, group_index):
        _, _, leave_w, carried = group_masks(group_index, doc_lengths, decays, GROUP)
        k_rows = k_all[group_index].astype(jnp.float32)
        v_rows = v_all[group_index].astype(jnp.float32)
        term = jnp.einsum('hj,jhd,jhe->hde', leave_w, k_rows, v_rows, precision=precise)
        return carried[:, None, None] * state + term, state

    def backward_step(future, group_index):
        _, enter_w, _, carried = group_masks(group_index, doc_lengths, decays, GROUP)
        q_rows = q_all[group_index].astype(jnp.float32)
        g_rows = g_all[group_index].astype(jnp.float32)
        term = jnp.einsum('hi,ihd,ihe->hde', enter_w, q_rows, g_rows, precision=precise)
        return carried[:, None, None] * future + term, future

    indices = jnp.arange(group_count, dtype=jnp.int32)
    empty_state = jnp.zeros((HEADS, DH, DH), jnp.float32)
    _, states = lax.scan(forward_step, empty_state, indices)
    _, futures = lax.scan(backward_step, empty_state, indices, reverse=True)

    def group_outputs(packed):
        group_index, state_in, state_next = packed
        weights, enter_w, leave_w, _ = group_masks(group_index, doc_lengths, decays, GROUP)
        q_rows = q_all[group_index].astype(jnp.float32)
        k_rows = k_all[group_index].astype(jnp.float32)
        v_rows = v_all[group_index].astype(jnp.float32)
        g_rows = g_all[group_index].astype(jnp.float32)
        enter_t = enter_w.T[:, :, None]
        leave_t = leave_w.T[:, :, None]
        scores = (jnp.einsum('ihd,jhd->hij', q_rows, k_rows, precision=precise) * weights).astype(jnp.bfloat16)
        scores = lax.optimization_barrier(scores).astype(jnp.float32)
        grads_loc = (jnp.einsum('ihd,jhd->hij', g_rows, v_rows, precision=precise) * weights).astype(jnp.bfloat16)
        grads_loc = lax.optimization_barrier(grads_loc).astype(jnp.float32)
        attended = jnp.einsum('hij,jhd->ihd', scores, v_rows, precision=precise) + jnp.einsum('ihd,hde->ihe', q_rows, state_in, precision=precise) * enter_t
        grad_q = jnp.einsum('hij,jhd->ihd', grads_loc, k_rows, precision=precise) + jnp.einsum('ihe,hde->ihd', g_rows, state_in, precision=precise) * enter_t
        grad_k = jnp.einsum('hij,ihd->jhd', grads_loc, q_rows, precision=precise) + jnp.einsum('jhe,hde->jhd', v_rows, state_next, precision=precise) * leave_t
        grad_v = jnp.einsum('hij,ihe->jhe', scores, g_rows, precision=precise) + jnp.einsum('jhd,hde->jhe', k_rows, state_next, precision=precise) * leave_t
        return (attended.astype(jnp.bfloat16), grad_q.astype(jnp.bfloat16), grad_k.astype(jnp.bfloat16), grad_v.astype(jnp.bfloat16))

    results = lax.map(group_outputs, (indices, states, futures))
    return (results[0].reshape(SEQ, HEADS * DH), results[1].reshape(SEQ, HEADS * DH), results[2].reshape(SEQ, HEADS * DH), results[3].reshape(SEQ, HEADS * DH))
```

```python
import jax
import jax.numpy as jnp
from jax import lax
from jax.sharding import PartitionSpec as P

DH = 128


def in_one_piece(arrays, axis, split_dim, concat_dim, along):
    widths = [a.shape[along] for a in arrays]
    both = jnp.concatenate(arrays, axis=along)
    out = lax.all_to_all(both, axis, split_axis=split_dim, concat_axis=concat_dim, tiled=True)
    return tuple(jnp.split(out, [sum(widths[:k]) for k in range(1, len(widths))], axis=along))


def segment_of(positions, doc_ends):
    return jnp.sum((doc_ends[None, :] <= positions[:, None]).astype(jnp.int32), axis=1)


def group_masks(group_index, doc_ends, decays, group_len):
    offsets = jnp.arange(group_len, dtype=jnp.int32)
    first_row = group_index * group_len
    segment = segment_of(first_row + offsets, doc_ends)
    segment_prev = segment_of(first_row - 1 + jnp.zeros((1,), jnp.int32), doc_ends)[0]
    segment_last = segment[group_len - 1]
    enters = (segment == segment_prev).astype(jnp.float32)
    leaves = (segment == segment_last).astype(jnp.float32)
    distance = (offsets[:, None] - offsets[None, :]).astype(jnp.float32)
    allowed = (offsets[:, None] >= offsets[None, :]) & (segment[:, None] == segment[None, :])
    weights = jnp.where(
        allowed[None], jnp.exp(-decays[:, None, None] * jnp.maximum(distance, 0.0)[None]), 0.0
    )
    offsets_f = offsets.astype(jnp.float32)
    enter_w = jnp.exp(-decays[:, None] * (offsets_f + 1.0)[None]) * enters[None]
    leave_w = jnp.exp(-decays[:, None] * (group_len - 1.0 - offsets_f)[None]) * leaves[None]
    return (weights, enter_w, leave_w)


def decayed_scan(term, anchors, here, decays, group_len, count, forward):
    total = term
    shift = 1
    while shift < count:
        if forward:
            pairs = [(i, i + shift) for i in range(count - shift)]
            other = jnp.maximum(here - shift, 0)
        else:
            pairs = [(i + shift, i) for i in range(count - shift)]
            other = jnp.minimum(here + shift, count - 1)
        incoming = lax.ppermute(total, "ctx", pairs)
        same = (anchors[here] == anchors[other]).astype(jnp.float32)
        factor = jnp.exp(-decays * float(group_len * shift)) * same
        total = total + factor[:, None, None] * incoming
        shift *= 2
    if forward:
        pairs = [(i, i + 1) for i in range(count - 1)]
    else:
        pairs = [(i + 1, i) for i in range(count - 1)]
    return lax.ppermute(total, "ctx", pairs)


def on_device(queries, keys, values, out_grad, decay_rate, doc_lengths):
    precise = lax.Precision.HIGHEST
    rows_in = queries.shape[0]
    count = lax.axis_size("ctx")
    group_len = rows_in * lax.axis_size("exp")
    here = lax.axis_index("ctx")
    doc_ends = jnp.cumsum(doc_lengths)
    weights, enter_w, leave_w = group_masks(here, doc_ends, decay_rate, group_len)
    starts = jnp.arange(count, dtype=jnp.int32) * group_len
    end_segments = segment_of(starts + (group_len - 1), doc_ends)
    before_segments = segment_of(starts - 1, doc_ends)
    q_rows, k_rows, v_rows, g_rows = in_one_piece(
        (
            queries.reshape(rows_in, -1, DH),
            keys.reshape(rows_in, -1, DH),
            values.reshape(rows_in, -1, DH),
            out_grad.reshape(rows_in, -1, DH),
        ),
        "exp",
        1,
        0,
        2,
    )
    k_wide = k_rows.astype(jnp.float32)
    v_wide = v_rows.astype(jnp.float32)
    q_wide = q_rows.astype(jnp.float32)
    g_wide = g_rows.astype(jnp.float32)
    enter_t = enter_w.T[:, :, None]
    leave_t = leave_w.T[:, :, None]
    forward_term = jnp.einsum("jhd,jhe->hde", k_wide * leave_t, v_wide, precision=precise)
    backward_term = jnp.einsum("ihd,ihe->hde", q_wide * enter_t, g_wide, precision=precise)
    state_in = decayed_scan(
        forward_term, end_segments, here, decay_rate, group_len, count, True
    )
    state_next = decayed_scan(
        backward_term, before_segments, here, decay_rate, group_len, count, False
    )
    scores = (
        jnp.einsum("ihd,jhd->hij", q_rows, k_rows, preferred_element_type=jnp.float32) * weights
    ).astype(jnp.bfloat16)
    grads_loc = (
        jnp.einsum("ihd,jhd->hij", g_rows, v_rows, preferred_element_type=jnp.float32) * weights
    ).astype(jnp.bfloat16)
    attended = jnp.einsum("hij,jhd->ihd", scores, v_rows, preferred_element_type=jnp.float32)
    grad_q = jnp.einsum("hij,jhd->ihd", grads_loc, k_rows, preferred_element_type=jnp.float32)
    grad_k = jnp.einsum("hij,ihd->jhd", grads_loc, q_rows, preferred_element_type=jnp.float32)
    grad_v = jnp.einsum("hij,ihe->jhe", scores, g_rows, preferred_element_type=jnp.float32)
    attended = (
        attended + jnp.einsum("ihd,hde->ihe", q_wide, state_in, precision=precise) * enter_t
    ).astype(jnp.bfloat16)
    grad_q = (
        grad_q + jnp.einsum("ihe,hde->ihd", g_wide, state_in, precision=precise) * enter_t
    ).astype(jnp.bfloat16)
    grad_k = (
        grad_k + jnp.einsum("jhe,hde->jhd", v_wide, state_next, precision=precise) * leave_t
    ).astype(jnp.bfloat16)
    grad_v = (
        grad_v + jnp.einsum("jhd,hde->jhe", k_wide, state_next, precision=precise) * leave_t
    ).astype(jnp.bfloat16)
    return (
        attended.reshape(group_len, -1),
        grad_q.reshape(group_len, -1),
        grad_k.reshape(group_len, -1),
        grad_v.reshape(group_len, -1),
    )


def solution(mesh):
    placed = (
        P(("ctx", "exp"), None),
        P(("ctx", "exp"), None),
        P(("ctx", "exp"), None),
        P(("ctx", "exp"), None),
        P("exp"),
        P(),
    )
    return jax.shard_map(
        on_device,
        mesh=mesh,
        in_specs=placed,
        out_specs=(P("ctx", "exp"), P("ctx", "exp"), P("ctx", "exp"), P("ctx", "exp")),
        check_vma=False,
    )
```

```python
import jax
import jax.numpy as jnp
from jax import lax
from jax.sharding import PartitionSpec as P

DH = 128


def in_one_piece(arrays, axis, split_dim, concat_dim, along):
    widths = [a.shape[along] for a in arrays]
    both = jnp.concatenate(arrays, axis=along)
    out = lax.all_to_all(both, axis, split_axis=split_dim, concat_axis=concat_dim, tiled=True)
    return tuple(jnp.split(out, [sum(widths[:k]) for k in range(1, len(widths))], axis=along))


def segment_of(positions, doc_ends):
    return jnp.sum((doc_ends[None, :] <= positions[:, None]).astype(jnp.int32), axis=1)


def group_masks(group_index, doc_ends, decays, group_len):
    offsets = jnp.arange(group_len, dtype=jnp.int32)
    first_row = group_index * group_len
    segment = segment_of(first_row + offsets, doc_ends)
    segment_prev = segment_of(first_row - 1 + jnp.zeros((1,), jnp.int32), doc_ends)[0]
    segment_last = segment[group_len - 1]
    enters = (segment == segment_prev).astype(jnp.float32)
    leaves = (segment == segment_last).astype(jnp.float32)
    distance = (offsets[:, None] - offsets[None, :]).astype(jnp.float32)
    allowed = (offsets[:, None] >= offsets[None, :]) & (segment[:, None] == segment[None, :])
    weights = jnp.where(
        allowed[None], jnp.exp(-decays[:, None, None] * jnp.maximum(distance, 0.0)[None]), 0.0
    )
    offsets_f = offsets.astype(jnp.float32)
    enter_w = jnp.exp(-decays[:, None] * (offsets_f + 1.0)[None]) * enters[None]
    leave_w = jnp.exp(-decays[:, None] * (group_len - 1.0 - offsets_f)[None]) * leaves[None]
    return (weights, enter_w, leave_w)


def decayed_scan(term, anchors, here, decays, group_len, count, forward, radix):
    def pull(value, shift):
        if forward:
            pairs = [(i, i + shift) for i in range(count - shift)]
        else:
            pairs = [(i + shift, i) for i in range(count - shift)]
        return lax.ppermute(value, "ctx", pairs)

    def anchor_at(offset):
        at = here - offset if forward else here + offset
        return anchors[jnp.clip(at, 0, count - 1)]

    mine = anchor_at(1)
    total = None
    for shift in range(1, min(radix, count - 1) + 1):
        same = (anchor_at(shift) == mine).astype(jnp.float32)
        factor = jnp.exp(-decays * float(group_len * (shift - 1))) * same
        part = factor[:, None, None] * pull(term, shift)
        total = part if total is None else total + part
    window = radix
    while window < count - 1:
        previous = total
        for step in range(1, radix):
            shift = window * step
            if shift >= count:
                break
            same = (anchor_at(shift + 1) == mine).astype(jnp.float32)
            factor = jnp.exp(-decays * float(group_len * shift)) * same
            total = total + factor[:, None, None] * pull(previous, shift)
        window *= radix
    return total


def on_device(queries, keys, values, out_grad, decay_rate, doc_lengths):
    precise = lax.Precision.HIGHEST
    rows_in = queries.shape[0]
    count = lax.axis_size("ctx")
    group_len = rows_in * lax.axis_size("exp")
    here = lax.axis_index("ctx")
    doc_ends = jnp.cumsum(doc_lengths)
    weights, enter_w, leave_w = group_masks(here, doc_ends, decay_rate, group_len)
    starts = jnp.arange(count, dtype=jnp.int32) * group_len
    end_segments = segment_of(starts + (group_len - 1), doc_ends)
    before_segments = segment_of(starts - 1, doc_ends)
    q_rows, k_rows, v_rows, g_rows = in_one_piece(
        (
            queries.reshape(rows_in, -1, DH),
            keys.reshape(rows_in, -1, DH),
            values.reshape(rows_in, -1, DH),
            out_grad.reshape(rows_in, -1, DH),
        ),
        "exp",
        1,
        0,
        2,
    )
    k_wide = k_rows.astype(jnp.float32)
    v_wide = v_rows.astype(jnp.float32)
    q_wide = q_rows.astype(jnp.float32)
    g_wide = g_rows.astype(jnp.float32)
    enter_t = enter_w.T[:, :, None]
    leave_t = leave_w.T[:, :, None]
    forward_term = jnp.einsum("jhd,jhe->hde", k_wide * leave_t, v_wide, precision=precise)
    backward_term = jnp.einsum("ihd,ihe->hde", q_wide * enter_t, g_wide, precision=precise)
    state_in = decayed_scan(
        forward_term, end_segments, here, decay_rate, group_len, count, True, 4
    )
    state_next = decayed_scan(
        backward_term, before_segments, here, decay_rate, group_len, count, False, 4
    )
    scores = (
        jnp.einsum("ihd,jhd->hij", q_rows, k_rows, preferred_element_type=jnp.float32) * weights
    ).astype(jnp.bfloat16)
    grads_loc = (
        jnp.einsum("ihd,jhd->hij", g_rows, v_rows, preferred_element_type=jnp.float32) * weights
    ).astype(jnp.bfloat16)
    attended = jnp.einsum("hij,jhd->ihd", scores, v_rows, preferred_element_type=jnp.float32)
    grad_q = jnp.einsum("hij,jhd->ihd", grads_loc, k_rows, preferred_element_type=jnp.float32)
    grad_k = jnp.einsum("hij,ihd->jhd", grads_loc, q_rows, preferred_element_type=jnp.float32)
    grad_v = jnp.einsum("hij,ihe->jhe", scores, g_rows, preferred_element_type=jnp.float32)
    attended = (
        attended + jnp.einsum("ihd,hde->ihe", q_wide, state_in, precision=precise) * enter_t
    ).astype(jnp.bfloat16)
    grad_q = (
        grad_q + jnp.einsum("ihe,hde->ihd", g_wide, state_in, precision=precise) * enter_t
    ).astype(jnp.bfloat16)
    grad_k = (
        grad_k + jnp.einsum("jhe,hde->jhd", v_wide, state_next, precision=precise) * leave_t
    ).astype(jnp.bfloat16)
    grad_v = (
        grad_v + jnp.einsum("jhd,hde->jhe", k_wide, state_next, precision=precise) * leave_t
    ).astype(jnp.bfloat16)
    return (
        attended.reshape(group_len, -1),
        grad_q.reshape(group_len, -1),
        grad_k.reshape(group_len, -1),
        grad_v.reshape(group_len, -1),
    )


def solution(mesh):
    placed = (
        P(("ctx", "exp"), None),
        P(("ctx", "exp"), None),
        P(("ctx", "exp"), None),
        P(("ctx", "exp"), None),
        P("exp"),
        P(),
    )
    return jax.shard_map(
        on_device,
        mesh=mesh,
        in_specs=placed,
        out_specs=(P("ctx", "exp"), P("ctx", "exp"), P("ctx", "exp"), P("ctx", "exp")),
        check_vma=False,
    )
```

```python
import jax
import jax.numpy as jnp
from jax import lax
from jax.sharding import PartitionSpec as P

DH = 128


def in_one_piece(arrays, axis, split_dim, concat_dim, along):
    widths = [a.shape[along] for a in arrays]
    both = jnp.concatenate(arrays, axis=along)
    out = lax.all_to_all(both, axis, split_axis=split_dim, concat_axis=concat_dim, tiled=True)
    return tuple(jnp.split(out, [sum(widths[:k]) for k in range(1, len(widths))], axis=along))


def segment_of(positions, doc_ends):
    return jnp.sum((doc_ends[None, :] <= positions[:, None]).astype(jnp.int32), axis=1)


def group_masks(group_index, doc_ends, decays, group_len):
    offsets = jnp.arange(group_len, dtype=jnp.int32)
    first_row = group_index * group_len
    segment = segment_of(first_row + offsets, doc_ends)
    segment_prev = segment_of(first_row - 1 + jnp.zeros((1,), jnp.int32), doc_ends)[0]
    segment_last = segment[group_len - 1]
    enters = (segment == segment_prev).astype(jnp.float32)
    leaves = (segment == segment_last).astype(jnp.float32)
    distance = (offsets[:, None] - offsets[None, :]).astype(jnp.float32)
    allowed = (offsets[:, None] >= offsets[None, :]) & (segment[:, None] == segment[None, :])
    weights = jnp.where(
        allowed[None], jnp.exp(-decays[:, None, None] * jnp.maximum(distance, 0.0)[None]), 0.0
    )
    offsets_f = offsets.astype(jnp.float32)
    enter_w = jnp.exp(-decays[:, None] * (offsets_f + 1.0)[None]) * enters[None]
    leave_w = jnp.exp(-decays[:, None] * (group_len - 1.0 - offsets_f)[None]) * leaves[None]
    return (weights, enter_w, leave_w)


def butterfly_scan(forward_term, backward_term, end_segments, before_segments, here, decays,
                   group_len, count):
    def clipped(table, index):
        return table[jnp.clip(index, 0, count - 1)]

    def decay(groups):
        return jnp.exp(-decays * (jnp.asarray(groups) * group_len).astype(jnp.float32))

    ahead = jnp.zeros_like(forward_term)
    behind = jnp.zeros_like(backward_term)
    total_f, total_b = forward_term, backward_term
    shift = 1
    while shift < count:
        last = shift * 2 >= count
        upper = (here // shift) % 2 == 1
        start = (here // shift) * shift
        other = jnp.where(upper, start - shift, start + shift)
        pairs = [(i, i ^ shift) for i in range(count)]
        if last:
            got = lax.ppermute(jnp.where(upper, total_b, total_f), "ctx", pairs)
            got_f = got_b = got
        else:
            got = lax.ppermute(jnp.stack([total_f, total_b]), "ctx", pairs)
            got_f, got_b = got[0], got[1]
        up = upper.astype(jnp.float32)
        to_ahead = decay(here - start) * (
            clipped(end_segments, start - 1) == clipped(end_segments, here - 1)
        ).astype(jnp.float32)
        ahead = ahead + (up * to_ahead)[:, None, None] * got_f
        to_behind = decay(start + shift - 1 - here) * (
            clipped(before_segments, start + shift) == clipped(before_segments, here + 1)
        ).astype(jnp.float32)
        behind = behind + ((1.0 - up) * to_behind)[:, None, None] * got_b
        if not last:
            joined_f = decay(shift) * (
                clipped(end_segments, start + shift - 1) == clipped(end_segments, other + shift - 1)
            ).astype(jnp.float32)
            joined_b = decay(shift) * (
                clipped(before_segments, start) == clipped(before_segments, other)
            ).astype(jnp.float32)
            total_f = jnp.where(upper, 1.0, joined_f)[:, None, None] * total_f + jnp.where(
                upper, joined_f, 1.0
            )[:, None, None] * got_f
            total_b = jnp.where(upper, joined_b, 1.0)[:, None, None] * total_b + jnp.where(
                upper, 1.0, joined_b
            )[:, None, None] * got_b
        shift *= 2
    return ahead, behind


def on_device(queries, keys, values, out_grad, decay_rate, doc_lengths):
    precise = lax.Precision.HIGHEST
    rows_in = queries.shape[0]
    count = lax.axis_size("ctx")
    group_len = rows_in * lax.axis_size("exp")
    here = lax.axis_index("ctx")
    doc_ends = jnp.cumsum(doc_lengths)
    weights, enter_w, leave_w = group_masks(here, doc_ends, decay_rate, group_len)
    starts = jnp.arange(count, dtype=jnp.int32) * group_len
    end_segments = segment_of(starts + (group_len - 1), doc_ends)
    before_segments = segment_of(starts - 1, doc_ends)
    q_rows, k_rows, v_rows, g_rows = in_one_piece(
        (
            queries.reshape(rows_in, -1, DH),
            keys.reshape(rows_in, -1, DH),
            values.reshape(rows_in, -1, DH),
            out_grad.reshape(rows_in, -1, DH),
        ),
        "exp",
        1,
        0,
        2,
    )
    k_wide = k_rows.astype(jnp.float32)
    v_wide = v_rows.astype(jnp.float32)
    q_wide = q_rows.astype(jnp.float32)
    g_wide = g_rows.astype(jnp.float32)
    enter_t = enter_w.T[:, :, None]
    leave_t = leave_w.T[:, :, None]
    forward_term = jnp.einsum("jhd,jhe->hde", k_wide * leave_t, v_wide, precision=precise)
    backward_term = jnp.einsum("ihd,ihe->hde", q_wide * enter_t, g_wide, precision=precise)
    state_in, state_next = butterfly_scan(
        forward_term, backward_term, end_segments, before_segments, here, decay_rate, group_len,
        count,
    )
    scores = (
        jnp.einsum("ihd,jhd->hij", q_rows, k_rows, preferred_element_type=jnp.float32) * weights
    ).astype(jnp.bfloat16)
    grads_loc = (
        jnp.einsum("ihd,jhd->hij", g_rows, v_rows, preferred_element_type=jnp.float32) * weights
    ).astype(jnp.bfloat16)
    attended = jnp.einsum("hij,jhd->ihd", scores, v_rows, preferred_element_type=jnp.float32)
    grad_q = jnp.einsum("hij,jhd->ihd", grads_loc, k_rows, preferred_element_type=jnp.float32)
    grad_k = jnp.einsum("hij,ihd->jhd", grads_loc, q_rows, preferred_element_type=jnp.float32)
    grad_v = jnp.einsum("hij,ihe->jhe", scores, g_rows, preferred_element_type=jnp.float32)
    attended = (
        attended + jnp.einsum("ihd,hde->ihe", q_wide, state_in, precision=precise) * enter_t
    ).astype(jnp.bfloat16)
    grad_q = (
        grad_q + jnp.einsum("ihe,hde->ihd", g_wide, state_in, precision=precise) * enter_t
    ).astype(jnp.bfloat16)
    grad_k = (
        grad_k + jnp.einsum("jhe,hde->jhd", v_wide, state_next, precision=precise) * leave_t
    ).astype(jnp.bfloat16)
    grad_v = (
        grad_v + jnp.einsum("jhd,hde->jhe", k_wide, state_next, precision=precise) * leave_t
    ).astype(jnp.bfloat16)
    return (
        attended.reshape(group_len, -1),
        grad_q.reshape(group_len, -1),
        grad_k.reshape(group_len, -1),
        grad_v.reshape(group_len, -1),
    )


def solution(mesh):
    placed = (
        P(("ctx", "exp"), None),
        P(("ctx", "exp"), None),
        P(("ctx", "exp"), None),
        P(("ctx", "exp"), None),
        P("exp"),
        P(),
    )
    return jax.shard_map(
        on_device,
        mesh=mesh,
        in_specs=placed,
        out_specs=(P("ctx", "exp"), P("ctx", "exp"), P("ctx", "exp"), P("ctx", "exp")),
        check_vma=False,
    )
```

```python
import jax
import jax.numpy as jnp
from jax import lax
from jax.sharding import PartitionSpec as P

DH = 128


def in_one_piece(arrays, axis, split_dim, concat_dim, along):
    widths = [a.shape[along] for a in arrays]
    both = jnp.concatenate(arrays, axis=along)
    out = lax.all_to_all(both, axis, split_axis=split_dim, concat_axis=concat_dim, tiled=True)
    return tuple(jnp.split(out, [sum(widths[:k]) for k in range(1, len(widths))], axis=along))


def segment_of(positions, doc_ends):
    return jnp.sum((doc_ends[None, :] <= positions[:, None]).astype(jnp.int32), axis=1)


def group_masks(group_index, doc_ends, decays, group_len):
    offsets = jnp.arange(group_len, dtype=jnp.int32)
    first_row = group_index * group_len
    segment = segment_of(first_row + offsets, doc_ends)
    segment_prev = segment_of(first_row - 1 + jnp.zeros((1,), jnp.int32), doc_ends)[0]
    segment_last = segment[group_len - 1]
    enters = (segment == segment_prev).astype(jnp.float32)
    leaves = (segment == segment_last).astype(jnp.float32)
    distance = (offsets[:, None] - offsets[None, :]).astype(jnp.float32)
    allowed = (offsets[:, None] >= offsets[None, :]) & (segment[:, None] == segment[None, :])
    weights = jnp.where(
        allowed[None], jnp.exp(-decays[:, None, None] * jnp.maximum(distance, 0.0)[None]), 0.0
    )
    offsets_f = offsets.astype(jnp.float32)
    enter_w = jnp.exp(-decays[:, None] * (offsets_f + 1.0)[None]) * enters[None]
    leave_w = jnp.exp(-decays[:, None] * (group_len - 1.0 - offsets_f)[None]) * leaves[None]
    return (weights, enter_w, leave_w)


def butterfly_scan(forward_term, backward_term, end_segments, before_segments, here, decays,
                   group_len, count):
    def clipped(table, index):
        return table[jnp.clip(index, 0, count - 1)]

    def decay(groups):
        return jnp.exp(-decays * (jnp.asarray(groups) * group_len).astype(jnp.float32))

    def column(factor):
        return factor[:, None, None]

    odd = here % 2 == 1
    ahead = jnp.zeros_like(forward_term)
    behind = jnp.zeros_like(backward_term)
    total_f, total_b = forward_term, backward_term
    shift = 1
    while shift < count:
        upper = (here // shift) % 2 == 1
        start = (here // shift) * shift
        other = jnp.where(upper, start - shift, start + shift)
        pairs = [(i, i ^ shift) for i in range(count)]
        if shift == 1:
            got = lax.ppermute(jnp.stack([total_f, total_b]), "ctx", pairs)
            got_f, got_b = got[0], got[1]
            use_f = use_b = jnp.ones((), jnp.float32)
        else:
            got_f = got_b = lax.ppermute(jnp.where(odd, total_b, total_f), "ctx", pairs)
            use_b = odd.astype(jnp.float32)
            use_f = 1.0 - use_b
        up = upper.astype(jnp.float32)
        to_ahead = decay(here - start) * (
            clipped(end_segments, start - 1) == clipped(end_segments, here - 1)
        ).astype(jnp.float32)
        ahead = ahead + column(use_f * up * to_ahead) * got_f
        to_behind = decay(start + shift - 1 - here) * (
            clipped(before_segments, start + shift) == clipped(before_segments, here + 1)
        ).astype(jnp.float32)
        behind = behind + column(use_b * (1.0 - up) * to_behind) * got_b
        if shift * 2 < count:
            joined_f = decay(shift) * (
                clipped(end_segments, start + shift - 1) == clipped(end_segments, other + shift - 1)
            ).astype(jnp.float32)
            joined_b = decay(shift) * (
                clipped(before_segments, start) == clipped(before_segments, other)
            ).astype(jnp.float32)
            total_f = column(jnp.where(upper, 1.0, joined_f)) * total_f + column(
                jnp.where(upper, joined_f, 1.0)
            ) * got_f
            total_b = column(jnp.where(upper, joined_b, 1.0)) * total_b + column(
                jnp.where(upper, 1.0, joined_b)
            ) * got_b
        shift *= 2
    if count > 2:
        got = lax.ppermute(jnp.where(odd, behind, ahead), "ctx", [(i, i ^ 1) for i in range(count)])
        move_f = decay(1) * (
            clipped(end_segments, here - 2) == clipped(end_segments, here - 1)
        ).astype(jnp.float32)
        move_b = decay(1) * (
            clipped(before_segments, here + 2) == clipped(before_segments, here + 1)
        ).astype(jnp.float32)
        oddf = odd.astype(jnp.float32)
        ahead = ahead + column(oddf * move_f) * got
        behind = behind + column((1.0 - oddf) * move_b) * got
    return ahead, behind


def on_device(queries, keys, values, out_grad, decay_rate, doc_lengths):
    precise = lax.Precision.HIGHEST
    rows_in = queries.shape[0]
    count = lax.axis_size("ctx")
    group_len = rows_in * lax.axis_size("exp")
    here = lax.axis_index("ctx")
    doc_ends = jnp.cumsum(doc_lengths)
    weights, enter_w, leave_w = group_masks(here, doc_ends, decay_rate, group_len)
    starts = jnp.arange(count, dtype=jnp.int32) * group_len
    end_segments = segment_of(starts + (group_len - 1), doc_ends)
    before_segments = segment_of(starts - 1, doc_ends)
    q_rows, k_rows, v_rows, g_rows = in_one_piece(
        (
            queries.reshape(rows_in, -1, DH),
            keys.reshape(rows_in, -1, DH),
            values.reshape(rows_in, -1, DH),
            out_grad.reshape(rows_in, -1, DH),
        ),
        "exp",
        1,
        0,
        2,
    )
    k_wide = k_rows.astype(jnp.float32)
    v_wide = v_rows.astype(jnp.float32)
    q_wide = q_rows.astype(jnp.float32)
    g_wide = g_rows.astype(jnp.float32)
    enter_t = enter_w.T[:, :, None]
    leave_t = leave_w.T[:, :, None]
    forward_term = jnp.einsum("jhd,jhe->hde", k_wide * leave_t, v_wide, precision=precise)
    backward_term = jnp.einsum("ihd,ihe->hde", q_wide * enter_t, g_wide, precision=precise)
    state_in, state_next = butterfly_scan(
        forward_term, backward_term, end_segments, before_segments, here, decay_rate, group_len,
        count,
    )
    scores = (
        jnp.einsum("ihd,jhd->hij", q_rows, k_rows, preferred_element_type=jnp.float32) * weights
    ).astype(jnp.bfloat16)
    grads_loc = (
        jnp.einsum("ihd,jhd->hij", g_rows, v_rows, preferred_element_type=jnp.float32) * weights
    ).astype(jnp.bfloat16)
    attended = jnp.einsum("hij,jhd->ihd", scores, v_rows, preferred_element_type=jnp.float32)
    grad_q = jnp.einsum("hij,jhd->ihd", grads_loc, k_rows, preferred_element_type=jnp.float32)
    grad_k = jnp.einsum("hij,ihd->jhd", grads_loc, q_rows, preferred_element_type=jnp.float32)
    grad_v = jnp.einsum("hij,ihe->jhe", scores, g_rows, preferred_element_type=jnp.float32)
    attended = (
        attended + jnp.einsum("ihd,hde->ihe", q_wide, state_in, precision=precise) * enter_t
    ).astype(jnp.bfloat16)
    grad_q = (
        grad_q + jnp.einsum("ihe,hde->ihd", g_wide, state_in, precision=precise) * enter_t
    ).astype(jnp.bfloat16)
    grad_k = (
        grad_k + jnp.einsum("jhe,hde->jhd", v_wide, state_next, precision=precise) * leave_t
    ).astype(jnp.bfloat16)
    grad_v = (
        grad_v + jnp.einsum("jhd,hde->jhe", k_wide, state_next, precision=precise) * leave_t
    ).astype(jnp.bfloat16)
    return (
        attended.reshape(group_len, -1),
        grad_q.reshape(group_len, -1),
        grad_k.reshape(group_len, -1),
        grad_v.reshape(group_len, -1),
    )


def solution(mesh):
    placed = (
        P(("ctx", "exp"), None),
        P(("ctx", "exp"), None),
        P(("ctx", "exp"), None),
        P(("ctx", "exp"), None),
        P("exp"),
        P(),
    )
    return jax.shard_map(
        on_device,
        mesh=mesh,
        in_specs=placed,
        out_specs=(P("ctx", "exp"), P("ctx", "exp"), P("ctx", "exp"), P("ctx", "exp")),
        check_vma=False,
    )
```

```python
import jax
import jax.numpy as jnp
from jax import lax
from jax.sharding import PartitionSpec as P

DH = 128


def in_one_piece(arrays, axis, split_dim, concat_dim, along):
    widths = [a.shape[along] for a in arrays]
    both = jnp.concatenate(arrays, axis=along)
    out = lax.all_to_all(both, axis, split_axis=split_dim, concat_axis=concat_dim, tiled=True)
    return tuple(jnp.split(out, [sum(widths[:k]) for k in range(1, len(widths))], axis=along))


def segment_of(positions, doc_ends):
    return jnp.sum((doc_ends[None, :] <= positions[:, None]).astype(jnp.int32), axis=1)


def group_masks(group_index, doc_ends, decays, group_len):
    offsets = jnp.arange(group_len, dtype=jnp.int32)
    first_row = group_index * group_len
    segment = segment_of(first_row + offsets, doc_ends)
    segment_prev = segment_of(first_row - 1 + jnp.zeros((1,), jnp.int32), doc_ends)[0]
    segment_last = segment[group_len - 1]
    enters = (segment == segment_prev).astype(jnp.float32)
    leaves = (segment == segment_last).astype(jnp.float32)
    distance = (offsets[:, None] - offsets[None, :]).astype(jnp.float32)
    allowed = (offsets[:, None] >= offsets[None, :]) & (segment[:, None] == segment[None, :])
    weights = jnp.where(
        allowed[None], jnp.exp(-decays[:, None, None] * jnp.maximum(distance, 0.0)[None]), 0.0
    )
    offsets_f = offsets.astype(jnp.float32)
    enter_w = jnp.exp(-decays[:, None] * (offsets_f + 1.0)[None]) * enters[None]
    leave_w = jnp.exp(-decays[:, None] * (group_len - 1.0 - offsets_f)[None]) * leaves[None]
    return (weights, enter_w, leave_w)


def butterfly_scan(forward_term, backward_term, end_segments, before_segments, here, decays,
                   group_len, count):
    def clipped(table, index):
        return table[jnp.clip(index, 0, count - 1)]

    def decay(groups):
        return jnp.exp(-decays * (jnp.asarray(groups) * group_len).astype(jnp.float32))

    def column(factor):
        return factor[:, None, None]

    odd = here % 2 == 1
    ahead = jnp.zeros_like(forward_term)
    behind = jnp.zeros_like(backward_term)
    total_f, total_b = forward_term, backward_term
    shift = 1
    while shift < count:
        upper = (here // shift) % 2 == 1
        start = (here // shift) * shift
        other = jnp.where(upper, start - shift, start + shift)
        pairs = [(i, i ^ shift) for i in range(count)]
        if shift == 1:
            got = lax.ppermute(jnp.stack([total_f, total_b]), "ctx", pairs)
            got_f, got_b = got[0], got[1]
            use_f = use_b = jnp.ones((), jnp.float32)
        else:
            got_f = got_b = lax.ppermute(jnp.where(odd, total_b, total_f), "ctx", pairs)
            use_b = odd.astype(jnp.float32)
            use_f = 1.0 - use_b
        up = upper.astype(jnp.float32)
        to_ahead = decay(here - start) * (
            clipped(end_segments, start - 1) == clipped(end_segments, here - 1)
        ).astype(jnp.float32)
        ahead = ahead + column(use_f * up * to_ahead) * got_f
        to_behind = decay(start + shift - 1 - here) * (
            clipped(before_segments, start + shift) == clipped(before_segments, here + 1)
        ).astype(jnp.float32)
        behind = behind + column(use_b * (1.0 - up) * to_behind) * got_b
        if shift * 2 < count:
            joined_f = decay(shift) * (
                clipped(end_segments, start + shift - 1) == clipped(end_segments, other + shift - 1)
            ).astype(jnp.float32)
            joined_b = decay(shift) * (
                clipped(before_segments, start) == clipped(before_segments, other)
            ).astype(jnp.float32)
            total_f = column(jnp.where(upper, 1.0, joined_f)) * total_f + column(
                jnp.where(upper, joined_f, 1.0)
            ) * got_f
            total_b = column(jnp.where(upper, joined_b, 1.0)) * total_b + column(
                jnp.where(upper, 1.0, joined_b)
            ) * got_b
        shift *= 2
    if count > 2:
        got = lax.ppermute(jnp.where(odd, behind, ahead), "ctx", [(i, i ^ 1) for i in range(count)])
        move_f = decay(1) * (
            clipped(end_segments, here - 2) == clipped(end_segments, here - 1)
        ).astype(jnp.float32)
        move_b = decay(1) * (
            clipped(before_segments, here + 2) == clipped(before_segments, here + 1)
        ).astype(jnp.float32)
        oddf = odd.astype(jnp.float32)
        ahead = ahead + column(oddf * move_f) * got
        behind = behind + column((1.0 - oddf) * move_b) * got
    return ahead, behind


def on_device(queries, keys, values, out_grad, decay_rate, doc_lengths):
    precise = lax.Precision.HIGHEST
    rows_in = queries.shape[0]
    count = lax.axis_size("ctx")
    group_len = rows_in * lax.axis_size("exp")
    here = lax.axis_index("ctx")
    doc_ends = jnp.cumsum(doc_lengths)
    weights, enter_w, leave_w = group_masks(here, doc_ends, decay_rate, group_len)
    starts = jnp.arange(count, dtype=jnp.int32) * group_len
    end_segments = segment_of(starts + (group_len - 1), doc_ends)
    before_segments = segment_of(starts - 1, doc_ends)
    moved = lax.all_to_all(
        jnp.stack([queries, keys, values, out_grad]), "exp", split_axis=2, concat_axis=1, tiled=True
    )
    heads = moved.shape[2] // DH
    rows = [
        tuple(moved[a, :, h * DH:(h + 1) * DH] for a in range(4)) for h in range(heads)
    ]
    forward_terms, backward_terms = [], []
    for h, (q, k, v, g) in enumerate(rows):
        forward_terms.append(
            jnp.dot(
                (k.astype(jnp.float32) * leave_w[h][:, None]).T,
                v.astype(jnp.float32),
                precision=precise,
            )
        )
        backward_terms.append(
            jnp.dot(
                (q.astype(jnp.float32) * enter_w[h][:, None]).T,
                g.astype(jnp.float32),
                precision=precise,
            )
        )
    state_in, state_next = butterfly_scan(
        jnp.stack(forward_terms), jnp.stack(backward_terms), end_segments, before_segments,
        here, decay_rate, group_len, count,
    )
    outs = [[], [], [], []]
    for h, (q, k, v, g) in enumerate(rows):
        wide = lambda x: x.astype(jnp.float32)
        scores = (
            jnp.dot(q, k.T, preferred_element_type=jnp.float32) * weights[h]
        ).astype(jnp.bfloat16)
        grads_loc = (
            jnp.dot(g, v.T, preferred_element_type=jnp.float32) * weights[h]
        ).astype(jnp.bfloat16)
        enter = enter_w[h][:, None]
        leave = leave_w[h][:, None]
        outs[0].append(
            jnp.dot(scores, v, preferred_element_type=jnp.float32)
            + jnp.dot(wide(q), state_in[h], precision=precise) * enter
        )
        outs[1].append(
            jnp.dot(grads_loc, k, preferred_element_type=jnp.float32)
            + jnp.dot(wide(g), state_in[h].T, precision=precise) * enter
        )
        outs[2].append(
            jnp.dot(grads_loc.T, q, preferred_element_type=jnp.float32)
            + jnp.dot(wide(v), state_next[h].T, precision=precise) * leave
        )
        outs[3].append(
            jnp.dot(scores.T, g, preferred_element_type=jnp.float32)
            + jnp.dot(wide(k), state_next[h], precision=precise) * leave
        )
    return tuple(jnp.concatenate(o, axis=1).astype(jnp.bfloat16) for o in outs)


def solution(mesh):
    placed = (
        P(("ctx", "exp"), None),
        P(("ctx", "exp"), None),
        P(("ctx", "exp"), None),
        P(("ctx", "exp"), None),
        P("exp"),
        P(),
    )
    return jax.shard_map(
        on_device,
        mesh=mesh,
        in_specs=placed,
        out_specs=(P("ctx", "exp"), P("ctx", "exp"), P("ctx", "exp"), P("ctx", "exp")),
        check_vma=False,
    )
```

```python
import jax
import jax.numpy as jnp
from jax import lax
from jax.sharding import PartitionSpec as P

DH = 128


def in_one_piece(arrays, axis, split_dim, concat_dim, along):
    widths = [a.shape[along] for a in arrays]
    both = jnp.concatenate(arrays, axis=along)
    out = lax.all_to_all(both, axis, split_axis=split_dim, concat_axis=concat_dim, tiled=True)
    return tuple(jnp.split(out, [sum(widths[:k]) for k in range(1, len(widths))], axis=along))


def segment_of(positions, doc_ends):
    return jnp.sum((doc_ends[None, :] <= positions[:, None]).astype(jnp.int32), axis=1)


def group_masks(group_index, doc_ends, decays, group_len):
    offsets = jnp.arange(group_len, dtype=jnp.int32)
    first_row = group_index * group_len
    segment = segment_of(first_row + offsets, doc_ends)
    segment_prev = segment_of(first_row - 1 + jnp.zeros((1,), jnp.int32), doc_ends)[0]
    segment_last = segment[group_len - 1]
    enters = (segment == segment_prev).astype(jnp.float32)
    leaves = (segment == segment_last).astype(jnp.float32)
    distance = (offsets[:, None] - offsets[None, :]).astype(jnp.float32)
    allowed = (offsets[:, None] >= offsets[None, :]) & (segment[:, None] == segment[None, :])
    weights = jnp.where(
        allowed[None], jnp.exp(-decays[:, None, None] * jnp.maximum(distance, 0.0)[None]), 0.0
    )
    offsets_f = offsets.astype(jnp.float32)
    enter_w = jnp.exp(-decays[:, None] * (offsets_f + 1.0)[None]) * enters[None]
    leave_w = jnp.exp(-decays[:, None] * (group_len - 1.0 - offsets_f)[None]) * leaves[None]
    return (weights, enter_w, leave_w)


def pair_scan(forward_term, backward_term, end_segments, before_segments, here, decays,
              group_len, count):
    def clipped(table, index):
        return table[jnp.clip(index, 0, count - 1)]

    def decay(groups):
        return jnp.exp(-decays * (jnp.asarray(groups) * group_len).astype(jnp.float32))

    def column(factor):
        return factor[:, None, None]

    def same(table, i, j):
        return (clipped(table, i) == clipped(table, j)).astype(jnp.float32)

    def push(value, pair_shift):
        shift = 2 * pair_shift
        pairs = [(i, i + shift) for i in range(0, count - shift, 2)]
        pairs += [(i, i - shift) for i in range(shift + 1, count, 2)]
        return lax.ppermute(value, "ctx", pairs)

    odd = here % 2 == 1
    partner = [(i, i ^ 1) for i in range(count)]
    mate = lax.ppermute(jnp.where(odd, forward_term, backward_term), "ctx", partner)
    pair_f = column(decay(1) * same(end_segments, here, here + 1)) * forward_term + mate
    pair_b = column(decay(1) * same(before_segments, here, here - 1)) * backward_term + mate
    pair_total = jnp.where(odd, pair_b, pair_f)
    def reach(pairs_away):
        groups = 2 * pairs_away
        forward = decay(groups) * same(end_segments, here - 1 - groups, here - 1)
        backward = decay(groups) * same(before_segments, here + 1 + groups, here + 1)
        return column(jnp.where(odd, backward, forward))

    total = push(pair_total, 1) + reach(1) * push(pair_total, 2)
    window = 2
    while window < count // 2:
        total = total + reach(window) * push(total, window)
        window *= 2
    handed_f = column(decay(1) * same(end_segments, here - 1, here)) * total + forward_term
    handed_b = column(decay(1) * same(before_segments, here + 1, here)) * total + backward_term
    handed = lax.ppermute(jnp.where(odd, handed_b, handed_f), "ctx", partner)
    return jnp.where(odd, handed, total), jnp.where(odd, total, handed)


def on_device(queries, keys, values, out_grad, decay_rate, doc_lengths):
    precise = lax.Precision.HIGHEST
    rows_in = queries.shape[0]
    count = lax.axis_size("ctx")
    group_len = rows_in * lax.axis_size("exp")
    here = lax.axis_index("ctx")
    doc_ends = jnp.cumsum(doc_lengths)
    weights, enter_w, leave_w = group_masks(here, doc_ends, decay_rate, group_len)
    starts = jnp.arange(count, dtype=jnp.int32) * group_len
    end_segments = segment_of(starts + (group_len - 1), doc_ends)
    before_segments = segment_of(starts - 1, doc_ends)
    q_rows, k_rows, v_rows, g_rows = in_one_piece(
        (
            queries.reshape(rows_in, -1, DH),
            keys.reshape(rows_in, -1, DH),
            values.reshape(rows_in, -1, DH),
            out_grad.reshape(rows_in, -1, DH),
        ),
        "exp",
        1,
        0,
        2,
    )
    k_wide = k_rows.astype(jnp.float32)
    v_wide = v_rows.astype(jnp.float32)
    q_wide = q_rows.astype(jnp.float32)
    g_wide = g_rows.astype(jnp.float32)
    enter_t = enter_w.T[:, :, None]
    leave_t = leave_w.T[:, :, None]
    forward_term = jnp.einsum("jhd,jhe->hde", k_wide * leave_t, v_wide, precision=precise)
    backward_term = jnp.einsum("ihd,ihe->hde", q_wide * enter_t, g_wide, precision=precise)
    state_in, state_next = pair_scan(
        forward_term, backward_term, end_segments, before_segments, here, decay_rate, group_len,
        count,
    )
    scores = (
        jnp.einsum("ihd,jhd->hij", q_rows, k_rows, preferred_element_type=jnp.float32) * weights
    ).astype(jnp.bfloat16)
    grads_loc = (
        jnp.einsum("ihd,jhd->hij", g_rows, v_rows, preferred_element_type=jnp.float32) * weights
    ).astype(jnp.bfloat16)
    attended = jnp.einsum("hij,jhd->ihd", scores, v_rows, preferred_element_type=jnp.float32)
    grad_q = jnp.einsum("hij,jhd->ihd", grads_loc, k_rows, preferred_element_type=jnp.float32)
    grad_k = jnp.einsum("hij,ihd->jhd", grads_loc, q_rows, preferred_element_type=jnp.float32)
    grad_v = jnp.einsum("hij,ihe->jhe", scores, g_rows, preferred_element_type=jnp.float32)
    attended = (
        attended + jnp.einsum("ihd,hde->ihe", q_wide, state_in, precision=precise) * enter_t
    ).astype(jnp.bfloat16)
    grad_q = (
        grad_q + jnp.einsum("ihe,hde->ihd", g_wide, state_in, precision=precise) * enter_t
    ).astype(jnp.bfloat16)
    grad_k = (
        grad_k + jnp.einsum("jhe,hde->jhd", v_wide, state_next, precision=precise) * leave_t
    ).astype(jnp.bfloat16)
    grad_v = (
        grad_v + jnp.einsum("jhd,hde->jhe", k_wide, state_next, precision=precise) * leave_t
    ).astype(jnp.bfloat16)
    return (
        attended.reshape(group_len, -1),
        grad_q.reshape(group_len, -1),
        grad_k.reshape(group_len, -1),
        grad_v.reshape(group_len, -1),
    )


def solution(mesh):
    placed = (
        P(("ctx", "exp"), None),
        P(("ctx", "exp"), None),
        P(("ctx", "exp"), None),
        P(("ctx", "exp"), None),
        P("exp"),
        P(),
    )
    return jax.shard_map(
        on_device,
        mesh=mesh,
        in_specs=placed,
        out_specs=(P("ctx", "exp"), P("ctx", "exp"), P("ctx", "exp"), P("ctx", "exp")),
        check_vma=False,
    )
```

```python
import jax
import jax.numpy as jnp
from jax import lax
from jax.sharding import PartitionSpec as P

DH = 128


def in_one_piece(arrays, axis, split_dim, concat_dim, along):
    widths = [a.shape[along] for a in arrays]
    both = jnp.concatenate(arrays, axis=along)
    out = lax.all_to_all(both, axis, split_axis=split_dim, concat_axis=concat_dim, tiled=True)
    return tuple(jnp.split(out, [sum(widths[:k]) for k in range(1, len(widths))], axis=along))


def segment_of(positions, doc_ends):
    return jnp.sum((doc_ends[None, :] <= positions[:, None]).astype(jnp.int32), axis=1)


def group_masks(group_index, doc_ends, decays, group_len):
    offsets = jnp.arange(group_len, dtype=jnp.int32)
    first_row = group_index * group_len
    segment = segment_of(first_row + offsets, doc_ends)
    segment_prev = segment_of(first_row - 1 + jnp.zeros((1,), jnp.int32), doc_ends)[0]
    segment_last = segment[group_len - 1]
    enters = (segment == segment_prev).astype(jnp.float32)
    leaves = (segment == segment_last).astype(jnp.float32)
    distance = (offsets[:, None] - offsets[None, :]).astype(jnp.float32)
    allowed = (offsets[:, None] >= offsets[None, :]) & (segment[:, None] == segment[None, :])
    weights = jnp.where(
        allowed[None], jnp.exp(-decays[:, None, None] * jnp.maximum(distance, 0.0)[None]), 0.0
    )
    offsets_f = offsets.astype(jnp.float32)
    enter_w = jnp.exp(-decays[:, None] * (offsets_f + 1.0)[None]) * enters[None]
    leave_w = jnp.exp(-decays[:, None] * (group_len - 1.0 - offsets_f)[None]) * leaves[None]
    return (weights, enter_w, leave_w)


def butterfly_scan(forward_term, backward_term, end_segments, before_segments, here, decays,
                   group_len, count):
    def clipped(table, index):
        return table[jnp.clip(index, 0, count - 1)]

    def decay(groups):
        return jnp.exp(-decays * (jnp.asarray(groups) * group_len).astype(jnp.float32))

    def column(factor):
        return factor[:, None, None]

    odd = here % 2 == 1
    ahead = jnp.zeros_like(forward_term)
    behind = jnp.zeros_like(backward_term)
    total_f, total_b = forward_term, backward_term
    shift = 1
    while shift < count:
        upper = (here // shift) % 2 == 1
        start = (here // shift) * shift
        other = jnp.where(upper, start - shift, start + shift)
        pairs = [(i, i ^ shift) for i in range(count)]
        if shift == 1:
            got = lax.ppermute(jnp.stack([total_f, total_b]), "ctx", pairs)
            got_f, got_b = got[0], got[1]
            use_f = use_b = jnp.ones((), jnp.float32)
        else:
            got_f = got_b = lax.ppermute(jnp.where(odd, total_b, total_f), "ctx", pairs)
            use_b = odd.astype(jnp.float32)
            use_f = 1.0 - use_b
        up = upper.astype(jnp.float32)
        to_ahead = decay(here - start) * (
            clipped(end_segments, start - 1) == clipped(end_segments, here - 1)
        ).astype(jnp.float32)
        ahead = ahead + column(use_f * up * to_ahead) * got_f
        to_behind = decay(start + shift - 1 - here) * (
            clipped(before_segments, start + shift) == clipped(before_segments, here + 1)
        ).astype(jnp.float32)
        behind = behind + column(use_b * (1.0 - up) * to_behind) * got_b
        if shift * 2 < count:
            joined_f = decay(shift) * (
                clipped(end_segments, start + shift - 1) == clipped(end_segments, other + shift - 1)
            ).astype(jnp.float32)
            joined_b = decay(shift) * (
                clipped(before_segments, start) == clipped(before_segments, other)
            ).astype(jnp.float32)
            total_f = column(jnp.where(upper, 1.0, joined_f)) * total_f + column(
                jnp.where(upper, joined_f, 1.0)
            ) * got_f
            total_b = column(jnp.where(upper, joined_b, 1.0)) * total_b + column(
                jnp.where(upper, 1.0, joined_b)
            ) * got_b
        shift *= 2
    if count > 2:
        got = lax.ppermute(jnp.where(odd, behind, ahead), "ctx", [(i, i ^ 1) for i in range(count)])
        move_f = decay(1) * (
            clipped(end_segments, here - 2) == clipped(end_segments, here - 1)
        ).astype(jnp.float32)
        move_b = decay(1) * (
            clipped(before_segments, here + 2) == clipped(before_segments, here + 1)
        ).astype(jnp.float32)
        oddf = odd.astype(jnp.float32)
        ahead = ahead + column(oddf * move_f) * got
        behind = behind + column((1.0 - oddf) * move_b) * got
    return ahead, behind


def on_device(queries, keys, values, out_grad, decay_rate, doc_lengths):
    precise = lax.Precision.HIGHEST
    rows_in = queries.shape[0]
    count = lax.axis_size("ctx")
    group_len = rows_in * lax.axis_size("exp")
    here = lax.axis_index("ctx")
    doc_ends = jnp.cumsum(doc_lengths)
    weights, enter_w, leave_w = group_masks(here, doc_ends, decay_rate, group_len)
    starts = jnp.arange(count, dtype=jnp.int32) * group_len
    end_segments = segment_of(starts + (group_len - 1), doc_ends)
    before_segments = segment_of(starts - 1, doc_ends)
    arrays = (queries, keys, values, out_grad)
    joined = jnp.concatenate(arrays, axis=0).reshape(len(arrays) * rows_in, -1, DH)
    moved = lax.all_to_all(joined, "exp", split_axis=1, concat_axis=0, tiled=True)
    moved = moved.reshape(-1, len(arrays), rows_in, moved.shape[1], DH)
    q_rows, k_rows, v_rows, g_rows = (
        moved[:, a].reshape(group_len, -1, DH) for a in range(len(arrays))
    )
    k_wide = k_rows.astype(jnp.float32)
    v_wide = v_rows.astype(jnp.float32)
    q_wide = q_rows.astype(jnp.float32)
    g_wide = g_rows.astype(jnp.float32)
    enter_t = enter_w.T[:, :, None]
    leave_t = leave_w.T[:, :, None]
    forward_term = jnp.einsum("jhd,jhe->hde", k_wide * leave_t, v_wide, precision=precise)
    backward_term = jnp.einsum("ihd,ihe->hde", q_wide * enter_t, g_wide, precision=precise)
    state_in, state_next = butterfly_scan(
        forward_term, backward_term, end_segments, before_segments, here, decay_rate, group_len,
        count,
    )
    scores = (
        jnp.einsum("ihd,jhd->hij", q_rows, k_rows, preferred_element_type=jnp.float32) * weights
    ).astype(jnp.bfloat16)
    grads_loc = (
        jnp.einsum("ihd,jhd->hij", g_rows, v_rows, preferred_element_type=jnp.float32) * weights
    ).astype(jnp.bfloat16)
    attended = jnp.einsum("hij,jhd->ihd", scores, v_rows, preferred_element_type=jnp.float32)
    grad_q = jnp.einsum("hij,jhd->ihd", grads_loc, k_rows, preferred_element_type=jnp.float32)
    grad_k = jnp.einsum("hij,ihd->jhd", grads_loc, q_rows, preferred_element_type=jnp.float32)
    grad_v = jnp.einsum("hij,ihe->jhe", scores, g_rows, preferred_element_type=jnp.float32)
    attended = (
        attended + jnp.einsum("ihd,hde->ihe", q_wide, state_in, precision=precise) * enter_t
    ).astype(jnp.bfloat16)
    grad_q = (
        grad_q + jnp.einsum("ihe,hde->ihd", g_wide, state_in, precision=precise) * enter_t
    ).astype(jnp.bfloat16)
    grad_k = (
        grad_k + jnp.einsum("jhe,hde->jhd", v_wide, state_next, precision=precise) * leave_t
    ).astype(jnp.bfloat16)
    grad_v = (
        grad_v + jnp.einsum("jhd,hde->jhe", k_wide, state_next, precision=precise) * leave_t
    ).astype(jnp.bfloat16)
    return (
        attended.reshape(group_len, -1),
        grad_q.reshape(group_len, -1),
        grad_k.reshape(group_len, -1),
        grad_v.reshape(group_len, -1),
    )


def solution(mesh):
    placed = (
        P(("ctx", "exp"), None),
        P(("ctx", "exp"), None),
        P(("ctx", "exp"), None),
        P(("ctx", "exp"), None),
        P("exp"),
        P(),
    )
    return jax.shard_map(
        on_device,
        mesh=mesh,
        in_specs=placed,
        out_specs=(P("ctx", "exp"), P("ctx", "exp"), P("ctx", "exp"), P("ctx", "exp")),
        check_vma=False,
    )
```

```python
import jax
import jax.numpy as jnp
from jax import lax
from jax.sharding import PartitionSpec as P

DH = 128


def in_one_piece(arrays, axis, split_dim, concat_dim, along):
    widths = [a.shape[along] for a in arrays]
    both = jnp.concatenate(arrays, axis=along)
    out = lax.all_to_all(both, axis, split_axis=split_dim, concat_axis=concat_dim, tiled=True)
    return tuple(jnp.split(out, [sum(widths[:k]) for k in range(1, len(widths))], axis=along))


def segment_of(positions, doc_ends):
    return jnp.sum((doc_ends[None, :] <= positions[:, None]).astype(jnp.int32), axis=1)


def group_masks(group_index, doc_ends, decays, group_len):
    offsets = jnp.arange(group_len, dtype=jnp.int32)
    first_row = group_index * group_len
    segment = segment_of(first_row + offsets, doc_ends)
    segment_prev = segment_of(first_row - 1 + jnp.zeros((1,), jnp.int32), doc_ends)[0]
    segment_last = segment[group_len - 1]
    enters = (segment == segment_prev).astype(jnp.float32)
    leaves = (segment == segment_last).astype(jnp.float32)
    distance = (offsets[:, None] - offsets[None, :]).astype(jnp.float32)
    allowed = (offsets[:, None] >= offsets[None, :]) & (segment[:, None] == segment[None, :])
    weights = jnp.where(
        allowed[None], jnp.exp(-decays[:, None, None] * jnp.maximum(distance, 0.0)[None]), 0.0
    )
    offsets_f = offsets.astype(jnp.float32)
    enter_w = jnp.exp(-decays[:, None] * (offsets_f + 1.0)[None]) * enters[None]
    leave_w = jnp.exp(-decays[:, None] * (group_len - 1.0 - offsets_f)[None]) * leaves[None]
    return (weights, enter_w, leave_w)


def butterfly_scan(forward_term, backward_term, end_segments, before_segments, here, decays,
                   group_len, count):
    def clipped(table, index):
        return table[jnp.clip(index, 0, count - 1)]

    def decay(groups):
        return jnp.exp(-decays * (jnp.asarray(groups) * group_len).astype(jnp.float32))

    def column(factor):
        return factor[:, None, None]

    odd = here % 2 == 1
    ahead = jnp.zeros_like(forward_term)
    behind = jnp.zeros_like(backward_term)
    total_f, total_b = forward_term, backward_term
    shift = 1
    while shift < count:
        upper = (here // shift) % 2 == 1
        start = (here // shift) * shift
        other = jnp.where(upper, start - shift, start + shift)
        pairs = [(i, i ^ shift) for i in range(count)]
        if shift == 1:
            got_f = got_b = lax.ppermute(jnp.where(odd, total_f, total_b), "ctx", pairs)
            use_f = use_b = jnp.zeros((), jnp.float32)
        else:
            got_f = got_b = lax.ppermute(jnp.where(odd, total_b, total_f), "ctx", pairs)
            use_b = odd.astype(jnp.float32)
            use_f = 1.0 - use_b
        up = upper.astype(jnp.float32)
        to_ahead = decay(here - start) * (
            clipped(end_segments, start - 1) == clipped(end_segments, here - 1)
        ).astype(jnp.float32)
        ahead = ahead + column(use_f * up * to_ahead) * got_f
        to_behind = decay(start + shift - 1 - here) * (
            clipped(before_segments, start + shift) == clipped(before_segments, here + 1)
        ).astype(jnp.float32)
        behind = behind + column(use_b * (1.0 - up) * to_behind) * got_b
        if shift * 2 < count:
            joined_f = decay(shift) * (
                clipped(end_segments, start + shift - 1) == clipped(end_segments, other + shift - 1)
            ).astype(jnp.float32)
            joined_b = decay(shift) * (
                clipped(before_segments, start) == clipped(before_segments, other)
            ).astype(jnp.float32)
            total_f = column(jnp.where(upper, 1.0, joined_f)) * total_f + column(
                jnp.where(upper, joined_f, 1.0)
            ) * got_f
            total_b = column(jnp.where(upper, joined_b, 1.0)) * total_b + column(
                jnp.where(upper, 1.0, joined_b)
            ) * got_b
        shift *= 2
    handed_f = column(decay(1) * (
        clipped(end_segments, here - 1) == clipped(end_segments, here)
    ).astype(jnp.float32)) * ahead + forward_term
    handed_b = column(decay(1) * (
        clipped(before_segments, here + 1) == clipped(before_segments, here)
    ).astype(jnp.float32)) * behind + backward_term
    got = lax.ppermute(
        jnp.where(odd, handed_b, handed_f), "ctx", [(i, i ^ 1) for i in range(count)]
    )
    return jnp.where(odd, got, ahead), jnp.where(odd, behind, got)


def on_device(queries, keys, values, out_grad, decay_rate, doc_lengths):
    precise = lax.Precision.HIGHEST
    rows_in = queries.shape[0]
    count = lax.axis_size("ctx")
    group_len = rows_in * lax.axis_size("exp")
    here = lax.axis_index("ctx")
    doc_ends = jnp.cumsum(doc_lengths)
    weights, enter_w, leave_w = group_masks(here, doc_ends, decay_rate, group_len)
    starts = jnp.arange(count, dtype=jnp.int32) * group_len
    end_segments = segment_of(starts + (group_len - 1), doc_ends)
    before_segments = segment_of(starts - 1, doc_ends)
    arrays = (queries, keys, values, out_grad)
    joined = jnp.concatenate(arrays, axis=0).reshape(len(arrays) * rows_in, -1, DH)
    moved = lax.all_to_all(joined, "exp", split_axis=1, concat_axis=0, tiled=True)
    moved = moved.reshape(-1, len(arrays), rows_in, moved.shape[1], DH)
    q_rows, k_rows, v_rows, g_rows = (
        moved[:, a].reshape(group_len, -1, DH) for a in range(len(arrays))
    )
    k_wide = k_rows.astype(jnp.float32)
    v_wide = v_rows.astype(jnp.float32)
    q_wide = q_rows.astype(jnp.float32)
    g_wide = g_rows.astype(jnp.float32)
    enter_t = enter_w.T[:, :, None]
    leave_t = leave_w.T[:, :, None]
    forward_term = jnp.einsum("jhd,jhe->hde", k_wide * leave_t, v_wide, precision=precise)
    backward_term = jnp.einsum("ihd,ihe->hde", q_wide * enter_t, g_wide, precision=precise)
    state_in, state_next = butterfly_scan(
        forward_term, backward_term, end_segments, before_segments, here, decay_rate, group_len,
        count,
    )
    scores = (
        jnp.einsum("ihd,jhd->hij", q_rows, k_rows, preferred_element_type=jnp.float32) * weights
    ).astype(jnp.bfloat16)
    grads_loc = (
        jnp.einsum("ihd,jhd->hij", g_rows, v_rows, preferred_element_type=jnp.float32) * weights
    ).astype(jnp.bfloat16)
    attended = jnp.einsum("hij,jhd->ihd", scores, v_rows, preferred_element_type=jnp.float32)
    grad_q = jnp.einsum("hij,jhd->ihd", grads_loc, k_rows, preferred_element_type=jnp.float32)
    grad_k = jnp.einsum("hij,ihd->jhd", grads_loc, q_rows, preferred_element_type=jnp.float32)
    grad_v = jnp.einsum("hij,ihe->jhe", scores, g_rows, preferred_element_type=jnp.float32)
    attended = (
        attended + jnp.einsum("ihd,hde->ihe", q_wide, state_in, precision=precise) * enter_t
    ).astype(jnp.bfloat16)
    grad_q = (
        grad_q + jnp.einsum("ihe,hde->ihd", g_wide, state_in, precision=precise) * enter_t
    ).astype(jnp.bfloat16)
    grad_k = (
        grad_k + jnp.einsum("jhe,hde->jhd", v_wide, state_next, precision=precise) * leave_t
    ).astype(jnp.bfloat16)
    grad_v = (
        grad_v + jnp.einsum("jhd,hde->jhe", k_wide, state_next, precision=precise) * leave_t
    ).astype(jnp.bfloat16)
    return (
        attended.reshape(group_len, -1),
        grad_q.reshape(group_len, -1),
        grad_k.reshape(group_len, -1),
        grad_v.reshape(group_len, -1),
    )


def solution(mesh):
    placed = (
        P(("ctx", "exp"), None),
        P(("ctx", "exp"), None),
        P(("ctx", "exp"), None),
        P(("ctx", "exp"), None),
        P("exp"),
        P(),
    )
    return jax.shard_map(
        on_device,
        mesh=mesh,
        in_specs=placed,
        out_specs=(P("ctx", "exp"), P("ctx", "exp"), P("ctx", "exp"), P("ctx", "exp")),
        check_vma=False,
    )
```

```python
import jax
import jax.numpy as jnp
from jax import lax
from jax.sharding import PartitionSpec as P

DH = 128


def in_one_piece(arrays, axis, split_dim, concat_dim, along):
    widths = [a.shape[along] for a in arrays]
    both = jnp.concatenate(arrays, axis=along)
    out = lax.all_to_all(both, axis, split_axis=split_dim, concat_axis=concat_dim, tiled=True)
    return tuple(jnp.split(out, [sum(widths[:k]) for k in range(1, len(widths))], axis=along))


def segment_of(positions, doc_ends):
    return jnp.sum((doc_ends[None, :] <= positions[:, None]).astype(jnp.int32), axis=1)


def group_masks(group_index, doc_ends, decays, group_len):
    offsets = jnp.arange(group_len, dtype=jnp.int32)
    first_row = group_index * group_len
    segment = segment_of(first_row + offsets, doc_ends)
    segment_prev = segment_of(first_row - 1 + jnp.zeros((1,), jnp.int32), doc_ends)[0]
    segment_last = segment[group_len - 1]
    enters = (segment == segment_prev).astype(jnp.float32)
    leaves = (segment == segment_last).astype(jnp.float32)
    distance = (offsets[:, None] - offsets[None, :]).astype(jnp.float32)
    allowed = (offsets[:, None] >= offsets[None, :]) & (segment[:, None] == segment[None, :])
    weights = jnp.where(
        allowed[None], jnp.exp(-decays[:, None, None] * jnp.maximum(distance, 0.0)[None]), 0.0
    )
    offsets_f = offsets.astype(jnp.float32)
    enter_w = jnp.exp(-decays[:, None] * (offsets_f + 1.0)[None]) * enters[None]
    leave_w = jnp.exp(-decays[:, None] * (group_len - 1.0 - offsets_f)[None]) * leaves[None]
    return (weights, enter_w, leave_w)


def butterfly_scan(forward_term, backward_term, sent_term, end_segments, before_segments, here,
                   decays, group_len, count):
    def clipped(table, index):
        return table[jnp.clip(index, 0, count - 1)]

    def decay(groups):
        return jnp.exp(-decays * (jnp.asarray(groups) * group_len).astype(jnp.float32))

    def column(factor):
        return factor[:, None, None]

    odd = here % 2 == 1
    ahead = jnp.zeros_like(forward_term)
    behind = jnp.zeros_like(backward_term)
    total_f, total_b = forward_term, backward_term
    shift = 1
    while shift < count:
        upper = (here // shift) % 2 == 1
        start = (here // shift) * shift
        other = jnp.where(upper, start - shift, start + shift)
        pairs = [(i, i ^ shift) for i in range(count)]
        if shift == 1:
            got_f = got_b = lax.ppermute(sent_term, "ctx", pairs)
            use_f = use_b = jnp.zeros((), jnp.float32)
        else:
            got_f = got_b = lax.ppermute(jnp.where(odd, total_b, total_f), "ctx", pairs)
            use_b = odd.astype(jnp.float32)
            use_f = 1.0 - use_b
        up = upper.astype(jnp.float32)
        to_ahead = decay(here - start) * (
            clipped(end_segments, start - 1) == clipped(end_segments, here - 1)
        ).astype(jnp.float32)
        ahead = ahead + column(use_f * up * to_ahead) * got_f
        to_behind = decay(start + shift - 1 - here) * (
            clipped(before_segments, start + shift) == clipped(before_segments, here + 1)
        ).astype(jnp.float32)
        behind = behind + column(use_b * (1.0 - up) * to_behind) * got_b
        if shift * 2 < count:
            joined_f = decay(shift) * (
                clipped(end_segments, start + shift - 1) == clipped(end_segments, other + shift - 1)
            ).astype(jnp.float32)
            joined_b = decay(shift) * (
                clipped(before_segments, start) == clipped(before_segments, other)
            ).astype(jnp.float32)
            total_f = column(jnp.where(upper, 1.0, joined_f)) * total_f + column(
                jnp.where(upper, joined_f, 1.0)
            ) * got_f
            total_b = column(jnp.where(upper, joined_b, 1.0)) * total_b + column(
                jnp.where(upper, 1.0, joined_b)
            ) * got_b
        shift *= 2
    handed_f = column(decay(1) * (
        clipped(end_segments, here - 1) == clipped(end_segments, here)
    ).astype(jnp.float32)) * ahead + forward_term
    handed_b = column(decay(1) * (
        clipped(before_segments, here + 1) == clipped(before_segments, here)
    ).astype(jnp.float32)) * behind + backward_term
    got = lax.ppermute(
        jnp.where(odd, handed_b, handed_f), "ctx", [(i, i ^ 1) for i in range(count)]
    )
    return jnp.where(odd, got, ahead), jnp.where(odd, behind, got)


def on_device(queries, keys, values, out_grad, decay_rate, doc_lengths):
    precise = lax.Precision.HIGH
    rows_in = queries.shape[0]
    count = lax.axis_size("ctx")
    group_len = rows_in * lax.axis_size("exp")
    here = lax.axis_index("ctx")
    doc_ends = jnp.cumsum(doc_lengths)
    weights, enter_w, leave_w = group_masks(here, doc_ends, decay_rate, group_len)
    starts = jnp.arange(count, dtype=jnp.int32) * group_len
    end_segments = segment_of(starts + (group_len - 1), doc_ends)
    before_segments = segment_of(starts - 1, doc_ends)
    arrays = (queries, keys, values, out_grad)
    joined = jnp.concatenate(arrays, axis=0).reshape(len(arrays) * rows_in, -1, DH)
    moved = lax.all_to_all(joined, "exp", split_axis=1, concat_axis=0, tiled=True)
    moved = moved.reshape(-1, len(arrays), rows_in, moved.shape[1], DH)
    q_rows, k_rows, v_rows, g_rows = (
        moved[:, a].reshape(group_len, -1, DH) for a in range(len(arrays))
    )
    k_wide = k_rows.astype(jnp.float32)
    v_wide = v_rows.astype(jnp.float32)
    q_wide = q_rows.astype(jnp.float32)
    g_wide = g_rows.astype(jnp.float32)
    enter_t = enter_w.T[:, :, None]
    leave_t = leave_w.T[:, :, None]
    odd = here % 2 == 1
    sent_term = jnp.einsum(
        "jhd,jhe->hde",
        jnp.where(odd, k_wide * leave_t, q_wide * enter_t),
        jnp.where(odd, v_wide, g_wide),
        precision=precise,
    )
    kept_term = jnp.einsum(
        "jhd,jhe->hde",
        jnp.where(odd, q_wide * enter_t, k_wide * leave_t),
        jnp.where(odd, g_wide, v_wide),
        precision=precise,
    )
    forward_term = jnp.where(odd, sent_term, kept_term)
    backward_term = jnp.where(odd, kept_term, sent_term)
    state_in, state_next = butterfly_scan(
        forward_term, backward_term, sent_term, end_segments, before_segments, here, decay_rate, group_len,
        count,
    )
    scores = (
        jnp.einsum("ihd,jhd->hij", q_rows, k_rows, preferred_element_type=jnp.float32) * weights
    ).astype(jnp.bfloat16)
    grads_loc = (
        jnp.einsum("ihd,jhd->hij", g_rows, v_rows, preferred_element_type=jnp.float32) * weights
    ).astype(jnp.bfloat16)
    attended = jnp.einsum("hij,jhd->ihd", scores, v_rows, preferred_element_type=jnp.float32)
    grad_q = jnp.einsum("hij,jhd->ihd", grads_loc, k_rows, preferred_element_type=jnp.float32)
    grad_k = jnp.einsum("hij,ihd->jhd", grads_loc, q_rows, preferred_element_type=jnp.float32)
    grad_v = jnp.einsum("hij,ihe->jhe", scores, g_rows, preferred_element_type=jnp.float32)
    attended = (
        attended + jnp.einsum("ihd,hde->ihe", q_wide, state_in, precision=precise) * enter_t
    ).astype(jnp.bfloat16)
    grad_q = (
        grad_q + jnp.einsum("ihe,hde->ihd", g_wide, state_in, precision=precise) * enter_t
    ).astype(jnp.bfloat16)
    grad_k = (
        grad_k + jnp.einsum("jhe,hde->jhd", v_wide, state_next, precision=precise) * leave_t
    ).astype(jnp.bfloat16)
    grad_v = (
        grad_v + jnp.einsum("jhd,hde->jhe", k_wide, state_next, precision=precise) * leave_t
    ).astype(jnp.bfloat16)
    return (
        attended.reshape(group_len, -1),
        grad_q.reshape(group_len, -1),
        grad_k.reshape(group_len, -1),
        grad_v.reshape(group_len, -1),
    )


def solution(mesh):
    placed = (
        P(("ctx", "exp"), None),
        P(("ctx", "exp"), None),
        P(("ctx", "exp"), None),
        P(("ctx", "exp"), None),
        P("exp"),
        P(),
    )
    return jax.shard_map(
        on_device,
        mesh=mesh,
        in_specs=placed,
        out_specs=(P("ctx", "exp"), P("ctx", "exp"), P("ctx", "exp"), P("ctx", "exp")),
        check_vma=False,
    )
```

```python
import jax
import jax.numpy as jnp
from jax import lax
from jax.sharding import PartitionSpec as P

DH = 128


def in_one_piece(arrays, axis, split_dim, concat_dim, along):
    widths = [a.shape[along] for a in arrays]
    both = jnp.concatenate(arrays, axis=along)
    out = lax.all_to_all(both, axis, split_axis=split_dim, concat_axis=concat_dim, tiled=True)
    return tuple(jnp.split(out, [sum(widths[:k]) for k in range(1, len(widths))], axis=along))


def segment_of(positions, doc_ends):
    return jnp.sum((doc_ends[None, :] <= positions[:, None]).astype(jnp.int32), axis=1)


def group_masks(group_index, doc_ends, decays, group_len):
    offsets = jnp.arange(group_len, dtype=jnp.int32)
    first_row = group_index * group_len
    segment = segment_of(first_row + offsets, doc_ends)
    segment_prev = segment_of(first_row - 1 + jnp.zeros((1,), jnp.int32), doc_ends)[0]
    segment_last = segment[group_len - 1]
    enters = (segment == segment_prev).astype(jnp.float32)
    leaves = (segment == segment_last).astype(jnp.float32)
    distance = (offsets[:, None] - offsets[None, :]).astype(jnp.float32)
    allowed = (offsets[:, None] >= offsets[None, :]) & (segment[:, None] == segment[None, :])
    weights = jnp.where(
        allowed[None], jnp.exp(-decays[:, None, None] * jnp.maximum(distance, 0.0)[None]), 0.0
    )
    offsets_f = offsets.astype(jnp.float32)
    enter_w = jnp.exp(-decays[:, None] * (offsets_f + 1.0)[None]) * enters[None]
    leave_w = jnp.exp(-decays[:, None] * (group_len - 1.0 - offsets_f)[None]) * leaves[None]
    return (weights, enter_w, leave_w)


def butterfly_scan(forward_term, backward_term, end_segments, before_segments, here, decays,
                   group_len, count):
    def clipped(table, index):
        return table[jnp.clip(index, 0, count - 1)]

    def decay(groups):
        return jnp.exp(-decays * (jnp.asarray(groups) * group_len).astype(jnp.float32))

    def column(factor):
        return factor[:, None, None]

    odd = here % 2 == 1
    ahead = jnp.zeros_like(forward_term)
    behind = jnp.zeros_like(backward_term)
    total_f, total_b = forward_term, backward_term
    shift = 1
    while shift < count:
        upper = (here // shift) % 2 == 1
        start = (here // shift) * shift
        other = jnp.where(upper, start - shift, start + shift)
        pairs = [(i, i ^ shift) for i in range(count)]
        if shift > 1 and shift * 2 >= count:
            pairs = [(i, j) for i, j in pairs if (i % 2 == 0) == (i < j)]
        if shift == 1:
            got = lax.ppermute(jnp.stack([total_f, total_b]), "ctx", pairs)
            got_f, got_b = got[0], got[1]
            use_f = use_b = jnp.ones((), jnp.float32)
        else:
            got_f = got_b = lax.ppermute(jnp.where(odd, total_b, total_f), "ctx", pairs)
            use_b = odd.astype(jnp.float32)
            use_f = 1.0 - use_b
        up = upper.astype(jnp.float32)
        to_ahead = decay(here - start) * (
            clipped(end_segments, start - 1) == clipped(end_segments, here - 1)
        ).astype(jnp.float32)
        ahead = ahead + column(use_f * up * to_ahead) * got_f
        to_behind = decay(start + shift - 1 - here) * (
            clipped(before_segments, start + shift) == clipped(before_segments, here + 1)
        ).astype(jnp.float32)
        behind = behind + column(use_b * (1.0 - up) * to_behind) * got_b
        if shift * 2 < count:
            joined_f = decay(shift) * (
                clipped(end_segments, start + shift - 1) == clipped(end_segments, other + shift - 1)
            ).astype(jnp.float32)
            joined_b = decay(shift) * (
                clipped(before_segments, start) == clipped(before_segments, other)
            ).astype(jnp.float32)
            total_f = column(jnp.where(upper, 1.0, joined_f)) * total_f + column(
                jnp.where(upper, joined_f, 1.0)
            ) * got_f
            total_b = column(jnp.where(upper, joined_b, 1.0)) * total_b + column(
                jnp.where(upper, 1.0, joined_b)
            ) * got_b
        shift *= 2
    if count > 2:
        got = lax.ppermute(jnp.where(odd, behind, ahead), "ctx", [(i, i ^ 1) for i in range(count)])
        move_f = decay(1) * (
            clipped(end_segments, here - 2) == clipped(end_segments, here - 1)
        ).astype(jnp.float32)
        move_b = decay(1) * (
            clipped(before_segments, here + 2) == clipped(before_segments, here + 1)
        ).astype(jnp.float32)
        oddf = odd.astype(jnp.float32)
        ahead = ahead + column(oddf * move_f) * got
        behind = behind + column((1.0 - oddf) * move_b) * got
    return ahead, behind


def on_device(queries, keys, values, out_grad, decay_rate, doc_lengths):
    precise = lax.Precision.HIGHEST
    rows_in = queries.shape[0]
    count = lax.axis_size("ctx")
    group_len = rows_in * lax.axis_size("exp")
    here = lax.axis_index("ctx")
    doc_ends = jnp.cumsum(doc_lengths)
    weights, enter_w, leave_w = group_masks(here, doc_ends, decay_rate, group_len)
    starts = jnp.arange(count, dtype=jnp.int32) * group_len
    end_segments = segment_of(starts + (group_len - 1), doc_ends)
    before_segments = segment_of(starts - 1, doc_ends)
    arrays = (queries, keys, values, out_grad)
    joined = jnp.concatenate(arrays, axis=0).reshape(len(arrays) * rows_in, -1, DH)
    moved = lax.all_to_all(joined, "exp", split_axis=1, concat_axis=0, tiled=True)
    moved = moved.reshape(-1, len(arrays), rows_in, moved.shape[1], DH)
    q_rows, k_rows, v_rows, g_rows = (
        moved[:, a].reshape(group_len, -1, DH) for a in range(len(arrays))
    )
    k_wide = k_rows.astype(jnp.float32)
    v_wide = v_rows.astype(jnp.float32)
    q_wide = q_rows.astype(jnp.float32)
    g_wide = g_rows.astype(jnp.float32)
    enter_t = enter_w.T[:, :, None]
    leave_t = leave_w.T[:, :, None]
    forward_term = jnp.einsum("jhd,jhe->hde", k_wide * leave_t, v_wide, precision=precise)
    backward_term = jnp.einsum("ihd,ihe->hde", q_wide * enter_t, g_wide, precision=precise)
    state_in, state_next = butterfly_scan(
        forward_term, backward_term, end_segments, before_segments, here, decay_rate, group_len,
        count,
    )
    scores = (
        jnp.einsum("ihd,jhd->hij", q_rows, k_rows, preferred_element_type=jnp.float32) * weights
    ).astype(jnp.bfloat16)
    grads_loc = (
        jnp.einsum("ihd,jhd->hij", g_rows, v_rows, preferred_element_type=jnp.float32) * weights
    ).astype(jnp.bfloat16)
    attended = jnp.einsum("hij,jhd->ihd", scores, v_rows, preferred_element_type=jnp.float32)
    grad_q = jnp.einsum("hij,jhd->ihd", grads_loc, k_rows, preferred_element_type=jnp.float32)
    grad_k = jnp.einsum("hij,ihd->jhd", grads_loc, q_rows, preferred_element_type=jnp.float32)
    grad_v = jnp.einsum("hij,ihe->jhe", scores, g_rows, preferred_element_type=jnp.float32)
    attended = (
        attended + jnp.einsum("ihd,hde->ihe", q_wide, state_in, precision=precise) * enter_t
    ).astype(jnp.bfloat16)
    grad_q = (
        grad_q + jnp.einsum("ihe,hde->ihd", g_wide, state_in, precision=precise) * enter_t
    ).astype(jnp.bfloat16)
    grad_k = (
        grad_k + jnp.einsum("jhe,hde->jhd", v_wide, state_next, precision=precise) * leave_t
    ).astype(jnp.bfloat16)
    grad_v = (
        grad_v + jnp.einsum("jhd,hde->jhe", k_wide, state_next, precision=precise) * leave_t
    ).astype(jnp.bfloat16)
    return (
        attended.reshape(group_len, -1),
        grad_q.reshape(group_len, -1),
        grad_k.reshape(group_len, -1),
        grad_v.reshape(group_len, -1),
    )


def solution(mesh):
    placed = (
        P(("ctx", "exp"), None),
        P(("ctx", "exp"), None),
        P(("ctx", "exp"), None),
        P(("ctx", "exp"), None),
        P("exp"),
        P(),
    )
    return jax.shard_map(
        on_device,
        mesh=mesh,
        in_specs=placed,
        out_specs=(P("ctx", "exp"), P("ctx", "exp"), P("ctx", "exp"), P("ctx", "exp")),
        check_vma=False,
    )
```

```python
import jax
import jax.numpy as jnp
from jax import lax
from jax.sharding import PartitionSpec as P

DH = 128


def in_one_piece(arrays, axis, split_dim, concat_dim, along):
    widths = [a.shape[along] for a in arrays]
    both = jnp.concatenate(arrays, axis=along)
    out = lax.all_to_all(both, axis, split_axis=split_dim, concat_axis=concat_dim, tiled=True)
    return tuple(jnp.split(out, [sum(widths[:k]) for k in range(1, len(widths))], axis=along))


def segment_of(positions, doc_ends):
    return jnp.sum((doc_ends[None, :] <= positions[:, None]).astype(jnp.int32), axis=1)


def group_masks(group_index, doc_ends, decays, group_len):
    offsets = jnp.arange(group_len, dtype=jnp.int32)
    first_row = group_index * group_len
    segment = segment_of(first_row + offsets, doc_ends)
    segment_prev = segment_of(first_row - 1 + jnp.zeros((1,), jnp.int32), doc_ends)[0]
    segment_last = segment[group_len - 1]
    enters = (segment == segment_prev).astype(jnp.float32)
    leaves = (segment == segment_last).astype(jnp.float32)
    distance = (offsets[:, None] - offsets[None, :]).astype(jnp.float32)
    allowed = (offsets[:, None] >= offsets[None, :]) & (segment[:, None] == segment[None, :])
    weights = jnp.where(
        allowed[None], jnp.exp(-decays[:, None, None] * jnp.maximum(distance, 0.0)[None]), 0.0
    )
    offsets_f = offsets.astype(jnp.float32)
    enter_w = jnp.exp(-decays[:, None] * (offsets_f + 1.0)[None]) * enters[None]
    leave_w = jnp.exp(-decays[:, None] * (group_len - 1.0 - offsets_f)[None]) * leaves[None]
    return (weights, enter_w, leave_w)


def butterfly_scan(forward_term, backward_term, end_segments, before_segments, here, decays,
                   group_len, count):
    def clipped(table, index):
        return table[jnp.clip(index, 0, count - 1)]

    def decay(groups):
        return jnp.exp(-decays * (jnp.asarray(groups) * group_len).astype(jnp.float32))

    def column(factor):
        return factor[:, None, None]

    odd = here % 2 == 1
    ahead = jnp.zeros_like(forward_term)
    behind = jnp.zeros_like(backward_term)
    total_f, total_b = forward_term, backward_term
    shift = 1
    while shift < count:
        upper = (here // shift) % 2 == 1
        start = (here // shift) * shift
        other = jnp.where(upper, start - shift, start + shift)
        pairs = [(i, i ^ shift) for i in range(count)]
        if shift > 1 and shift * 2 >= count:
            pairs = [(i, j) for i, j in pairs if (i % 2 == 0) == (i < j)]
        elif shift > 1 and shift * 4 == count:
            half = count // 2
            pairs = [
                (i, j)
                for i, j in pairs
                if (j % 2 == 0 and (j > i or j < half)) or (j % 2 == 1 and (j < i or j >= half))
            ]
        if shift == 1:
            got = lax.ppermute(jnp.stack([total_f, total_b]), "ctx", pairs)
            got_f, got_b = got[0], got[1]
            use_f = use_b = jnp.ones((), jnp.float32)
        else:
            got_f = got_b = lax.ppermute(jnp.where(odd, total_b, total_f), "ctx", pairs)
            use_b = odd.astype(jnp.float32)
            use_f = 1.0 - use_b
        up = upper.astype(jnp.float32)
        to_ahead = decay(here - start) * (
            clipped(end_segments, start - 1) == clipped(end_segments, here - 1)
        ).astype(jnp.float32)
        ahead = ahead + column(use_f * up * to_ahead) * got_f
        to_behind = decay(start + shift - 1 - here) * (
            clipped(before_segments, start + shift) == clipped(before_segments, here + 1)
        ).astype(jnp.float32)
        behind = behind + column(use_b * (1.0 - up) * to_behind) * got_b
        if shift * 2 < count:
            joined_f = decay(shift) * (
                clipped(end_segments, start + shift - 1) == clipped(end_segments, other + shift - 1)
            ).astype(jnp.float32)
            joined_b = decay(shift) * (
                clipped(before_segments, start) == clipped(before_segments, other)
            ).astype(jnp.float32)
            total_f = column(jnp.where(upper, 1.0, joined_f)) * total_f + column(
                jnp.where(upper, joined_f, 1.0)
            ) * got_f
            total_b = column(jnp.where(upper, joined_b, 1.0)) * total_b + column(
                jnp.where(upper, 1.0, joined_b)
            ) * got_b
        shift *= 2
    if count > 2:
        got = lax.ppermute(jnp.where(odd, behind, ahead), "ctx", [(i, i ^ 1) for i in range(count)])
        move_f = decay(1) * (
            clipped(end_segments, here - 2) == clipped(end_segments, here - 1)
        ).astype(jnp.float32)
        move_b = decay(1) * (
            clipped(before_segments, here + 2) == clipped(before_segments, here + 1)
        ).astype(jnp.float32)
        oddf = odd.astype(jnp.float32)
        ahead = ahead + column(oddf * move_f) * got
        behind = behind + column((1.0 - oddf) * move_b) * got
    return ahead, behind


def on_device(queries, keys, values, out_grad, decay_rate, doc_lengths):
    precise = lax.Precision.HIGHEST
    rows_in = queries.shape[0]
    count = lax.axis_size("ctx")
    group_len = rows_in * lax.axis_size("exp")
    here = lax.axis_index("ctx")
    doc_ends = jnp.cumsum(doc_lengths)
    weights, enter_w, leave_w = group_masks(here, doc_ends, decay_rate, group_len)
    starts = jnp.arange(count, dtype=jnp.int32) * group_len
    end_segments = segment_of(starts + (group_len - 1), doc_ends)
    before_segments = segment_of(starts - 1, doc_ends)
    arrays = (queries, keys, values, out_grad)
    joined = jnp.concatenate(arrays, axis=0).reshape(len(arrays) * rows_in, -1, DH)
    moved = lax.all_to_all(joined, "exp", split_axis=1, concat_axis=0, tiled=True)
    moved = moved.reshape(-1, len(arrays), rows_in, moved.shape[1], DH)
    q_rows, k_rows, v_rows, g_rows = (
        moved[:, a].reshape(group_len, -1, DH) for a in range(len(arrays))
    )
    k_wide = k_rows.astype(jnp.float32)
    v_wide = v_rows.astype(jnp.float32)
    q_wide = q_rows.astype(jnp.float32)
    g_wide = g_rows.astype(jnp.float32)
    enter_t = enter_w.T[:, :, None]
    leave_t = leave_w.T[:, :, None]
    forward_term = jnp.einsum("jhd,jhe->hde", k_wide * leave_t, v_wide, precision=precise)
    backward_term = jnp.einsum("ihd,ihe->hde", q_wide * enter_t, g_wide, precision=precise)
    state_in, state_next = butterfly_scan(
        forward_term, backward_term, end_segments, before_segments, here, decay_rate, group_len,
        count,
    )
    scores = (
        jnp.einsum("ihd,jhd->hij", q_rows, k_rows, preferred_element_type=jnp.float32) * weights
    ).astype(jnp.bfloat16)
    grads_loc = (
        jnp.einsum("ihd,jhd->hij", g_rows, v_rows, preferred_element_type=jnp.float32) * weights
    ).astype(jnp.bfloat16)
    attended = jnp.einsum("hij,jhd->ihd", scores, v_rows, preferred_element_type=jnp.float32)
    grad_q = jnp.einsum("hij,jhd->ihd", grads_loc, k_rows, preferred_element_type=jnp.float32)
    grad_k = jnp.einsum("hij,ihd->jhd", grads_loc, q_rows, preferred_element_type=jnp.float32)
    grad_v = jnp.einsum("hij,ihe->jhe", scores, g_rows, preferred_element_type=jnp.float32)
    attended = (
        attended + jnp.einsum("ihd,hde->ihe", q_wide, state_in, precision=precise) * enter_t
    ).astype(jnp.bfloat16)
    grad_q = (
        grad_q + jnp.einsum("ihe,hde->ihd", g_wide, state_in, precision=precise) * enter_t
    ).astype(jnp.bfloat16)
    grad_k = (
        grad_k + jnp.einsum("jhe,hde->jhd", v_wide, state_next, precision=precise) * leave_t
    ).astype(jnp.bfloat16)
    grad_v = (
        grad_v + jnp.einsum("jhd,hde->jhe", k_wide, state_next, precision=precise) * leave_t
    ).astype(jnp.bfloat16)
    return (
        attended.reshape(group_len, -1),
        grad_q.reshape(group_len, -1),
        grad_k.reshape(group_len, -1),
        grad_v.reshape(group_len, -1),
    )


def solution(mesh):
    placed = (
        P(("ctx", "exp"), None),
        P(("ctx", "exp"), None),
        P(("ctx", "exp"), None),
        P(("ctx", "exp"), None),
        P("exp"),
        P(),
    )
    return jax.shard_map(
        on_device,
        mesh=mesh,
        in_specs=placed,
        out_specs=(P("ctx", "exp"), P("ctx", "exp"), P("ctx", "exp"), P("ctx", "exp")),
        check_vma=False,
    )
```

```python
import jax
import jax.numpy as jnp
from jax import lax
from jax.sharding import PartitionSpec as P

DH = 128


def in_one_piece(arrays, axis, split_dim, concat_dim, along):
    widths = [a.shape[along] for a in arrays]
    both = jnp.concatenate(arrays, axis=along)
    out = lax.all_to_all(both, axis, split_axis=split_dim, concat_axis=concat_dim, tiled=True)
    return tuple(jnp.split(out, [sum(widths[:k]) for k in range(1, len(widths))], axis=along))


def segment_of(positions, doc_ends):
    return jnp.sum((doc_ends[None, :] <= positions[:, None]).astype(jnp.int32), axis=1)


def group_masks(group_index, doc_ends, decays, group_len):
    offsets = jnp.arange(group_len, dtype=jnp.int32)
    first_row = group_index * group_len
    segment = segment_of(first_row + offsets, doc_ends)
    segment_prev = segment_of(first_row - 1 + jnp.zeros((1,), jnp.int32), doc_ends)[0]
    segment_last = segment[group_len - 1]
    enters = (segment == segment_prev).astype(jnp.float32)
    leaves = (segment == segment_last).astype(jnp.float32)
    distance = (offsets[:, None] - offsets[None, :]).astype(jnp.float32)
    allowed = (offsets[:, None] >= offsets[None, :]) & (segment[:, None] == segment[None, :])
    weights = jnp.where(
        allowed[None], jnp.exp(-decays[:, None, None] * jnp.maximum(distance, 0.0)[None]), 0.0
    )
    offsets_f = offsets.astype(jnp.float32)
    enter_w = jnp.exp(-decays[:, None] * (offsets_f + 1.0)[None]) * enters[None]
    leave_w = jnp.exp(-decays[:, None] * (group_len - 1.0 - offsets_f)[None]) * leaves[None]
    return (weights, enter_w, leave_w)


def butterfly_scan(forward_term, backward_term, end_segments, before_segments, here, decays,
                   group_len, count):
    def clipped(table, index):
        return table[jnp.clip(index, 0, count - 1)]

    def decay(groups):
        return jnp.exp(-decays * (jnp.asarray(groups) * group_len).astype(jnp.float32))

    def column(factor):
        return factor[:, None, None]

    odd = here % 2 == 1
    ahead = jnp.zeros_like(forward_term)
    behind = jnp.zeros_like(backward_term)
    total_f, total_b = forward_term, backward_term
    shift = 1
    while shift < count:
        upper = (here // shift) % 2 == 1
        start = (here // shift) * shift
        other = jnp.where(upper, start - shift, start + shift)
        pairs = [(i, i ^ shift) for i in range(count)]
        if shift > 1 and shift * 2 >= count:
            pairs = [(i, j) for i, j in pairs if (i % 2 == 0) == (i < j)]
        if shift == 1:
            got = lax.ppermute(jnp.stack([total_f, total_b]), "ctx", pairs)
            got_f, got_b = got[0], got[1]
            use_f = use_b = jnp.ones((), jnp.float32)
        else:
            got_f = got_b = lax.ppermute(jnp.where(odd, total_b, total_f), "ctx", pairs)
            use_b = odd.astype(jnp.float32)
            use_f = 1.0 - use_b
        up = upper.astype(jnp.float32)
        to_ahead = decay(here - start) * (
            clipped(end_segments, start - 1) == clipped(end_segments, here - 1)
        ).astype(jnp.float32)
        ahead = ahead + column(use_f * up * to_ahead) * got_f
        to_behind = decay(start + shift - 1 - here) * (
            clipped(before_segments, start + shift) == clipped(before_segments, here + 1)
        ).astype(jnp.float32)
        behind = behind + column(use_b * (1.0 - up) * to_behind) * got_b
        if shift * 2 < count:
            joined_f = decay(shift) * (
                clipped(end_segments, start + shift - 1) == clipped(end_segments, other + shift - 1)
            ).astype(jnp.float32)
            joined_b = decay(shift) * (
                clipped(before_segments, start) == clipped(before_segments, other)
            ).astype(jnp.float32)
            total_f = column(jnp.where(upper, 1.0, joined_f)) * total_f + column(
                jnp.where(upper, joined_f, 1.0)
            ) * got_f
            total_b = column(jnp.where(upper, joined_b, 1.0)) * total_b + column(
                jnp.where(upper, 1.0, joined_b)
            ) * got_b
        shift *= 2
    if count > 2:
        got = lax.ppermute(jnp.where(odd, behind, ahead), "ctx", [(i, i ^ 1) for i in range(count)])
        move_f = decay(1) * (
            clipped(end_segments, here - 2) == clipped(end_segments, here - 1)
        ).astype(jnp.float32)
        move_b = decay(1) * (
            clipped(before_segments, here + 2) == clipped(before_segments, here + 1)
        ).astype(jnp.float32)
        oddf = odd.astype(jnp.float32)
        ahead = ahead + column(oddf * move_f) * got
        behind = behind + column((1.0 - oddf) * move_b) * got
    return ahead, behind


def on_device(queries, keys, values, out_grad, decay_rate, doc_lengths):
    precise = lax.Precision.HIGH
    rows_in = queries.shape[0]
    count = lax.axis_size("ctx")
    group_len = rows_in * lax.axis_size("exp")
    here = lax.axis_index("ctx")
    doc_ends = jnp.cumsum(doc_lengths)
    weights, enter_w, leave_w = group_masks(here, doc_ends, decay_rate, group_len)
    starts = jnp.arange(count, dtype=jnp.int32) * group_len
    end_segments = segment_of(starts + (group_len - 1), doc_ends)
    before_segments = segment_of(starts - 1, doc_ends)
    arrays = (queries, keys, values, out_grad)
    joined = jnp.concatenate(arrays, axis=0).reshape(len(arrays) * rows_in, -1, DH)
    moved = lax.all_to_all(joined, "exp", split_axis=1, concat_axis=0, tiled=True)
    moved = moved.reshape(-1, len(arrays), rows_in, moved.shape[1], DH)
    q_rows, k_rows, v_rows, g_rows = (
        moved[:, a].reshape(group_len, -1, DH) for a in range(len(arrays))
    )
    k_wide = k_rows.astype(jnp.float32)
    v_wide = v_rows.astype(jnp.float32)
    q_wide = q_rows.astype(jnp.float32)
    g_wide = g_rows.astype(jnp.float32)
    enter_t = enter_w.T[:, :, None]
    leave_t = leave_w.T[:, :, None]
    forward_term = jnp.einsum("jhd,jhe->hde", k_wide * leave_t, v_wide, precision=precise)
    backward_term = jnp.einsum("ihd,ihe->hde", q_wide * enter_t, g_wide, precision=precise)
    state_in, state_next = butterfly_scan(
        forward_term, backward_term, end_segments, before_segments, here, decay_rate, group_len,
        count,
    )
    scores = (
        jnp.einsum("ihd,jhd->hij", q_rows, k_rows, preferred_element_type=jnp.float32) * weights
    ).astype(jnp.bfloat16)
    grads_loc = (
        jnp.einsum("ihd,jhd->hij", g_rows, v_rows, preferred_element_type=jnp.float32) * weights
    ).astype(jnp.bfloat16)
    attended = jnp.einsum("hij,jhd->ihd", scores, v_rows, preferred_element_type=jnp.float32)
    grad_q = jnp.einsum("hij,jhd->ihd", grads_loc, k_rows, preferred_element_type=jnp.float32)
    grad_k = jnp.einsum("hij,ihd->jhd", grads_loc, q_rows, preferred_element_type=jnp.float32)
    grad_v = jnp.einsum("hij,ihe->jhe", scores, g_rows, preferred_element_type=jnp.float32)
    attended = (
        attended + jnp.einsum("ihd,hde->ihe", q_wide, state_in, precision=precise) * enter_t
    ).astype(jnp.bfloat16)
    grad_q = (
        grad_q + jnp.einsum("ihe,hde->ihd", g_wide, state_in, precision=precise) * enter_t
    ).astype(jnp.bfloat16)
    grad_k = (
        grad_k + jnp.einsum("jhe,hde->jhd", v_wide, state_next, precision=precise) * leave_t
    ).astype(jnp.bfloat16)
    grad_v = (
        grad_v + jnp.einsum("jhd,hde->jhe", k_wide, state_next, precision=precise) * leave_t
    ).astype(jnp.bfloat16)
    return (
        attended.reshape(group_len, -1),
        grad_q.reshape(group_len, -1),
        grad_k.reshape(group_len, -1),
        grad_v.reshape(group_len, -1),
    )


def solution(mesh):
    placed = (
        P(("ctx", "exp"), None),
        P(("ctx", "exp"), None),
        P(("ctx", "exp"), None),
        P(("ctx", "exp"), None),
        P("exp"),
        P(),
    )
    return jax.shard_map(
        on_device,
        mesh=mesh,
        in_specs=placed,
        out_specs=(P("ctx", "exp"), P("ctx", "exp"), P("ctx", "exp"), P("ctx", "exp")),
        check_vma=False,
    )
```
